32 devices in a mesh: attn: 8 (over z, y), exp: 4 (over x, core).
Axes of the slice: x: 2, y: 2, z: 4, core: 2. Of those that a mesh axis runs over, the one named last changes fastest.
Arguments:
- q_latent: bfloat16 [16, 128, 512], P('attn'), may hold values from -6 to 6
- q_rope: bfloat16 [16, 64, 128], P('attn'), may hold values from -8 to 8
- cache_latent: bfloat16 [16, 4096, 512], P('attn', 'exp'), may hold values from -6 to 6
- cache_rope: bfloat16 [16, 64, 4096], P('attn', None, 'exp'), may hold values from -8 to 8
- lengths: int32 [16], P('attn'), may hold values from 2 to 4096, as said below
- tokens: bfloat16 [256, 7168], P(('attn', 'exp')), may hold values from -6 to 6
- route_ids: int32 [256, 4], P(('attn', 'exp')), may hold values from 0 to 7, all different within a row; in each aligned block of 8 rows (0 to 7, 8 to 15, ...) at most 8 rows name the same one
- route_gates: float32 [256, 4], P(('attn', 'exp')), may hold values from 0.2 to 1
- w_gate: bfloat16 [8, 7168, 1024], P('attn', None, 'exp'), may hold values from -0.0625 to 0.0625
- w_up: bfloat16 [8, 7168, 1024], P('attn', None, 'exp'), may hold values from -0.0625 to 0.0625
- w_down: bfloat16 [8, 1024, 7168], P('attn', 'exp'), may hold values from -0.1875 to 0.1875
Outputs:
- attn_out: bfloat16 [16, 128, 512], P('attn', 'exp')
- moe_out: bfloat16 [256, 7168], P(('attn', 'exp'))
The draws below stay inside these ranges and needn't reach their ends.
Inputs may be any that keep to these rules, and one draw needn't show every extreme that they name: `route_ids`: within the rows of one device (aligned blocks of 8 rows) an expert is named at most 8 times; a token names 4 distinct experts. `lengths`: some request has length exactly 4096.
All inputs are finite; a program needn't handle non-finite values.
Results may differ from the reference program's by a relative error of at most 0.0058.
Values may be sent and summed in bfloat16 or wider, within the bound.
No kernel may reach another device: no remote copies, remote signals or barrier semaphores. Data moves between devices by JAX's collectives and lax.ppermute only.
A program may use at most 128 MiB of HBM per device.

```python
import math
import jax
import jax.numpy as jnp
import numpy as np
from jax import lax

D = 7168
HEADS = 128
LAT = 512
ROPE = 64
HID = 1024
TOP = 4
CTX = 4096
TOK_DEV = 8
POS_DEV = 1024
ROWS = 16
TOKENS = 256
EXPERTS = 8
CAP = 8
N_ATTN = 8
N_EXP = 4


def draw_q_latent(key, part):
    arr_shape = (ROWS, HEADS, LAT)
    draw_base = jax.random.normal(jax.random.fold_in(key, 11), arr_shape, jnp.float32)
    return jnp.clip(draw_base, -6.0, 6.0).astype(jnp.bfloat16)


def draw_q_rope(key, part):
    arr_shape = (ROWS, ROPE, HEADS)
    draw_base = jnp.clip(jax.random.normal(jax.random.fold_in(key, 21), arr_shape, jnp.float32), -6.0, 6.0)
    return jnp.clip(draw_base, -8.0, 8.0).astype(jnp.bfloat16)


def draw_cache_latent(key, part):
    arr_shape = (ROWS, CTX, LAT)
    draw_base = jax.random.normal(jax.random.fold_in(key, 41), arr_shape, jnp.float32)
    return jnp.clip(draw_base, -6.0, 6.0).astype(jnp.bfloat16)


def draw_cache_rope(key, part):
    arr_shape = (ROWS, ROPE, CTX)
    draw_base = jnp.clip(jax.random.normal(jax.random.fold_in(key, 51), arr_shape, jnp.float32), -6.0, 6.0)
    return jnp.clip(draw_base, -8.0, 8.0).astype(jnp.bfloat16)


def draw_lengths(key, part):
    drawn_lengths = jax.random.randint(jax.random.fold_in(key, 31), (ROWS,), 2, CTX + 1)
    full_row = jax.random.randint(jax.random.fold_in(key, 32), (), 0, ROWS)
    return jnp.where(jnp.arange(ROWS) == full_row, CTX, drawn_lengths).astype(jnp.int32)


def steps_of(stream_key, shape, split, low, high):
    level = 1.0
    for axis_at, shards_of in split:
        steps = jax.random.uniform(jax.random.fold_in(jax.random.fold_in(stream_key, 6), axis_at), (shards_of,), jnp.float32, low / len(split), high / len(split))
        level = level * jnp.repeat(jnp.exp(steps), shape[axis_at] // shards_of).reshape((-1,) + (1,) * (len(shape) - 1 - axis_at))
    return level


def assign_block(stream_key, own, number, rows, count, top, limit, lean):
    sequence = jax.random.permutation(stream_key, count)
    heavy_load, usual = shares(count, rows * top, limit, lean, True), shares(count, rows * top, limit, lean, False)
    places = jnp.arange(count)

    def named(sizes, turn):
        used = int((sizes > 0).sum())
        fixed = max(1, used // 4)
        shifted = fixed + (places - fixed + turn * (used - fixed)) % max(1, count - fixed)
        return jnp.zeros((count,), jnp.int32).at[sequence[jnp.where(places < fixed, places, shifted)]].set(jnp.asarray(sizes, jnp.int32))

    sizes = jnp.where(number % 4 == 0, named(heavy_load, number // 4), named(usual, number - number // 4 - 1))
    mixed = jax.random.permutation(jax.random.fold_in(own, 3), count)
    giver, taker = mixed[0:count // 2 * 2:2], mixed[1:count // 2 * 2:2]
    room = jnp.minimum(sizes[giver] - 1, limit - sizes[taker]) // 2
    room = jnp.where((giver == sequence[0]) | (taker == sequence[0]) | (sizes[taker] == 0), 0, jnp.maximum(room, 0))
    shifted = jax.random.randint(jax.random.fold_in(own, 4), (count // 2,), 0, 1 << 20) % (room + 1)
    sizes = sizes.at[giver].add(-shifted).at[taker].add(shifted)
    members = jnp.searchsorted(jnp.cumsum(sizes), jnp.arange(rows * top), side="right").astype(jnp.int32)
    grid = members.reshape(top, rows).T
    grid = grid[jax.random.permutation(jax.random.fold_in(own, 1), rows)]
    turn = jax.random.randint(jax.random.fold_in(own, 2), (rows, 1), 0, top)
    return jnp.take_along_axis(grid, (jnp.arange(top)[None, :] + turn) % top, axis=1)


def shares(amount, total, bound, slope, full):
    weights = [(1 << 20) // math.isqrt(rank ** slope) + 1 for rank in range(1, amount + 1)]
    largest = bound if full else min(bound, max(-(-total // amount), total * weights[0] // sum(weights)))
    least = 1 if total - largest >= amount - 1 else 0
    counts, surplus = [largest] + [least] * (amount - 1), total - largest - least * (amount - 1)
    while surplus > 0:
        candidates = [i for i in range(1, amount) if counts[i] < largest] or [i for i in range(1, amount) if counts[i] < bound]
        mass, budget = sum([weights[i] for i in candidates]), surplus
        for i in candidates:
            extra = min(bound - counts[i], max(1, budget * weights[i] // mass), surplus)
            counts[i] = counts[i] + extra
            surplus = surplus - extra
    return np.array(counts)


def gaussian(key, extent, scale, most, cuts=(), held_as=jnp.bfloat16):
    result = scale * jax.random.normal(key, extent, jnp.float32)
    if cuts:
        result = result * steps_of(key, extent, cuts, -0.22, 0.18)
    return jnp.clip(result, -most, most).astype(held_as)


def setup_inputs(seed: int = 0) -> dict:
    key_of = jax.random.split(jax.random.key(seed), 12)
    q_latent = draw_q_latent(jax.random.fold_in(key_of[11], 71), 0)
    q_rope = draw_q_rope(jax.random.fold_in(key_of[11], 71), 0)
    cache_latent = draw_cache_latent(jax.random.fold_in(key_of[11], 71), 0)
    cache_rope = draw_cache_rope(jax.random.fold_in(key_of[11], 71), 0)
    lengths = draw_lengths(jax.random.fold_in(key_of[11], 71), 0)
    tokens = gaussian(key_of[5], (TOKENS, D), 1.0, 6.0, ((0, 32),))
    route_ids_keys = jax.random.split(jax.random.fold_in(key_of[6], 1), TOKENS // TOK_DEV)
    route_ids_turns = jax.random.permutation(jax.random.fold_in(key_of[6], 3), TOKENS // TOK_DEV)
    route_ids = jax.vmap(lambda own, number: assign_block(jax.random.fold_in(key_of[6], 2), own, number, TOK_DEV, EXPERTS, TOP, CAP, 2))(route_ids_keys, route_ids_turns).reshape((TOKENS, TOP))
    route_gates = jnp.clip(0.2 + 0.8 * jax.random.uniform(key_of[7], (TOKENS, TOP), jnp.float32) ** steps_of(key_of[7], (TOKENS, TOP), ((0, 32),), -0.2, 0.2), 0.2, 1.0)
    w_gate = gaussian(key_of[8], (EXPERTS, D, HID), D ** -0.5, 0.0625, ((0, 8), (2, 4)))
    w_up = gaussian(key_of[9], (EXPERTS, D, HID), D ** -0.5, 0.0625, ((0, 8), (2, 4)))
    w_down = gaussian(key_of[10], (EXPERTS, HID, D), HID ** -0.5, 0.1875, ((0, 8), (1, 4)))
    return dict(q_latent=q_latent, q_rope=q_rope, cache_latent=cache_latent, cache_rope=cache_rope, lengths=lengths, tokens=tokens, route_ids=route_ids, route_gates=route_gates, w_gate=w_gate, w_up=w_up, w_down=w_down)


score_scale = 1.0 / math.sqrt(192.0)
neg_fill = -1e+30

def attend_row(pieces):
    q_lat, q_rot, c_lat, k_rot, length = pieces
    scores = jnp.dot(q_lat, c_lat.T, preferred_element_type=jnp.float32)
    scores = scores + jnp.dot(q_rot.T, k_rot, preferred_element_type=jnp.float32)
    scores = score_scale * scores
    is_live = jnp.arange(CTX, dtype=jnp.int32) < length
    masked = jnp.where(is_live[None, :], scores, neg_fill)
    blocks = masked.reshape(HEADS, N_EXP, POS_DEV)
    live_blocks = is_live.reshape(N_EXP, POS_DEV)[None, :, :]
    block_max = lax.optimization_barrier(jnp.max(blocks, axis=2))
    weights = jnp.where(live_blocks, jnp.exp(blocks - block_max[:, :, None]), 0.0)
    block_sum = lax.optimization_barrier(jnp.sum(weights, axis=2))
    rounded = lax.optimization_barrier(weights.astype(jnp.bfloat16))
    values = c_lat.reshape(N_EXP, POS_DEV, LAT)
    block_out = jnp.einsum('hbp,bpl->hbl', rounded.astype(jnp.float32), values.astype(jnp.float32))
    row_top = lax.optimization_barrier(jnp.max(block_max, axis=1))
    factor = jnp.exp(block_max - row_top[:, None])
    numerator = lax.optimization_barrier(jnp.sum(block_out * factor[:, :, None], axis=1))
    denominator = lax.optimization_barrier(jnp.sum(block_sum * factor, axis=1))
    return (numerator / denominator[:, None]).astype(jnp.bfloat16)

def reference(q_latent, q_rope, cache_latent, cache_rope, lengths, tokens, route_ids, route_gates, w_gate, w_up, w_down):
    attn_out = lax.map(attend_row, (q_latent, q_rope, cache_latent, cache_rope, lengths))
    row_limit = N_ATTN * N_EXP * CAP

    def one_expert(running, expert):
        is_hit = route_ids == expert
        weight = lax.optimization_barrier(jnp.sum(jnp.where(is_hit, route_gates, 0.0), axis=1))
        chosen = jnp.any(is_hit, axis=1)
        row_index = jnp.nonzero(chosen, size=row_limit, fill_value=0)[0].astype(jnp.int32)
        is_valid = jnp.arange(row_limit, dtype=jnp.int32) < jnp.sum(chosen.astype(jnp.int32))
        row_block = tokens[row_index]
        gate_value = jnp.dot(row_block, w_gate[expert], preferred_element_type=jnp.float32)
        up_value = jnp.dot(row_block, w_up[expert], preferred_element_type=jnp.float32)
        hidden = (jax.nn.silu(gate_value) * up_value).astype(jnp.bfloat16)
        expert_out = lax.optimization_barrier(jnp.dot(hidden, w_down[expert], preferred_element_type=jnp.float32).astype(jnp.bfloat16))
        row_weight = jnp.where(is_valid, weight[row_index], 0.0)
        running = running.at[row_index].add(row_weight[:, None] * expert_out.astype(jnp.float32))
        return (running, None)
    start_sum = jnp.zeros((TOKENS, D), jnp.float32)
    moe_sum, _ = lax.scan(one_expert, start_sum, jnp.arange(EXPERTS, dtype=jnp.int32))
    return (attn_out, moe_sum.astype(jnp.bfloat16))
```

```python
import math

import jax
import jax.numpy as jnp
from jax import lax
from jax.sharding import PartitionSpec as P

score_scale = 1.0 / math.sqrt(192.0)
neg_fill = -1e30


def expert_part(row_block, gate_slice, up_slice, down_slice):
    gate_value = jnp.dot(row_block, gate_slice, preferred_element_type=jnp.float32)
    upward = jnp.dot(row_block, up_slice, preferred_element_type=jnp.float32)
    hidden = (jax.nn.silu(gate_value) * upward).astype(jnp.bfloat16)
    return jnp.dot(hidden, down_slice, preferred_element_type=jnp.float32)


def per_device(
    q_latent,
    q_rope,
    cache_latent,
    cache_rope,
    lengths,
    tokens,
    route_ids,
    route_gates,
    w_gate,
    w_up,
    w_down,
):
    n_exp = lax.axis_size("exp")
    n_attn = lax.axis_size("attn")
    positions = cache_latent.shape[1]
    scores = jnp.einsum("rhl,rpl->rhp", q_latent, cache_latent, preferred_element_type=jnp.float32)
    scores = scores + jnp.einsum(
        "rdh,rdp->rhp", q_rope, cache_rope, preferred_element_type=jnp.float32
    )
    scores = score_scale * scores
    global_pos = lax.axis_index("exp") * positions + jnp.arange(positions, dtype=jnp.int32)
    is_live = global_pos[None, None, :] < lengths[:, None, None]
    masked = jnp.where(is_live, scores, neg_fill)
    block_max = jnp.max(masked, axis=2)
    weights = jnp.where(is_live, jnp.exp(masked - block_max[:, :, None]), 0.0)
    block_sum = jnp.sum(weights, axis=2)
    block_out = jnp.einsum(
        "rhp,rpl->rhl",
        weights.astype(jnp.bfloat16),
        cache_latent,
        preferred_element_type=jnp.float32,
    )
    row_top = lax.pmax(block_max, "exp")
    factor = jnp.exp(block_max - row_top)
    numerator, denominator = (
        lax.psum_scatter(block_out * factor[:, :, None], "exp", scatter_dimension=1, tiled=True),
        lax.psum_scatter(block_sum * factor, "exp", scatter_dimension=1, tiled=True),
    )
    attn_out = (numerator / denominator[:, :, None]).astype(jnp.bfloat16)
    n_local = w_gate.shape[0]
    all_axes = ("attn", "exp")
    tok_all = lax.all_gather(tokens, all_axes, axis=0, tiled=True)
    ids_all = lax.all_gather(route_ids, all_axes, axis=0, tiled=True)
    gates_all = lax.all_gather(route_gates, all_axes, axis=0, tiled=True)
    first_expert = lax.axis_index("attn") * n_local
    partial = None
    for i in range(n_local):
        weight = jnp.sum(jnp.where(ids_all == first_expert + i, gates_all, 0.0), axis=1)
        piece = expert_part(tok_all, w_gate[i], w_up[i], w_down[i]) * weight[:, None]
        partial = piece if partial is None else partial + piece
    moe_out = lax.psum_scatter(partial, all_axes, scatter_dimension=0, tiled=True).astype(
        jnp.bfloat16
    )
    return (attn_out, moe_out)


def solution(mesh):
    return jax.shard_map(
        per_device,
        mesh=mesh,
        in_specs=(
            P("attn", None, None),
            P("attn", None, None),
            P("attn", "exp", None),
            P("attn", None, "exp"),
            P("attn"),
            P(("attn", "exp"), None),
            P(("attn", "exp"), None),
            P(("attn", "exp"), None),
            P("attn", None, "exp"),
            P("attn", None, "exp"),
            P("attn", "exp", None),
        ),
        out_specs=(P("attn", "exp", None), P(("attn", "exp"), None)),
        check_vma=False,
    )
```

```python
import math

import jax
import jax.numpy as jnp
from jax import lax
from jax.sharding import PartitionSpec as P

score_scale = 1.0 / math.sqrt(192.0)
neg_fill = -1e30


def expert_part(row_block, gate_slice, up_slice, down_slice):
    gate_value = jnp.dot(row_block, gate_slice, preferred_element_type=jnp.float32)
    upward = jnp.dot(row_block, up_slice, preferred_element_type=jnp.float32)
    hidden = (jax.nn.silu(gate_value) * upward).astype(jnp.bfloat16)
    return jnp.dot(hidden, down_slice, preferred_element_type=jnp.float32)


def shift_gather(x, axis, n):
    pieces = [x]
    for k in range(1, n):
        pieces.append(lax.ppermute(x, axis, [(i, (i + k) % n) for i in range(n)]))
    return jnp.stack(pieces)


def shift_scatter_sum(q, axis, n):
    total = q[0]
    for k in range(1, n):
        total = total + lax.ppermute(q[k], axis, [(i, (i - k) % n) for i in range(n)])
    return total


def bit_gather(x, axis, bit, n):
    other = lax.ppermute(x, axis, [(i, i ^ bit) for i in range(n)])
    return jnp.stack([x, other])


def bit_reduce(x, axis, bit, n):
    return x[0] + lax.ppermute(x[1], axis, [(i, i ^ bit) for i in range(n)])


def routed_experts(tokens, route_ids, route_gates, w_gate, w_up, w_down):
    n_exp = lax.axis_size("exp")
    n_attn = lax.axis_size("attn")
    n_local = w_gate.shape[0]
    n_experts = n_attn * n_local
    tok_count, model_width = tokens.shape
    bits = []
    b = n_exp // 2
    while b >= 1:
        bits.append(b)
        b //= 2
    hit = route_ids[:, :, None] == jnp.arange(n_experts, dtype=jnp.int32)[None, None, :]
    wmat = jnp.sum(jnp.where(hit, route_gates[:, :, None], 0.0), axis=1)
    rows = shift_gather(tokens, "attn", n_attn)
    wrows = shift_gather(wmat, "attn", n_attn)
    for bit in bits:
        rows = bit_gather(rows, "exp", bit, n_exp)
        wrows = bit_gather(wrows, "exp", bit, n_exp)
    lead_shape = rows.shape[:-1]
    flat_rows = rows.reshape(-1, model_width)
    flat_w = wrows.reshape(-1, n_experts)
    first_expert = lax.axis_index("attn") * n_local
    result = None
    for i in range(n_local):
        partial = expert_part(flat_rows, w_gate[i], w_up[i], w_down[i])
        partial = partial.reshape(lead_shape + (model_width,))
        for bit in reversed(bits):
            partial = bit_reduce(partial, "exp", bit, n_exp)
        weight = lax.dynamic_index_in_dim(flat_w, first_expert + i, axis=1, keepdims=False)
        weight = weight.reshape(lead_shape)
        for _ in bits:
            weight = weight[0]
        piece = partial.astype(jnp.bfloat16).astype(jnp.float32) * weight[..., None]
        result = piece if result is None else result + piece
    return shift_scatter_sum(result, "attn", n_attn).astype(jnp.bfloat16)


def per_device(
    q_latent,
    q_rope,
    cache_latent,
    cache_rope,
    lengths,
    tokens,
    route_ids,
    route_gates,
    w_gate,
    w_up,
    w_down,
):
    n_exp = lax.axis_size("exp")
    n_attn = lax.axis_size("attn")
    positions = cache_latent.shape[1]
    scores = jnp.einsum("rhl,rpl->rhp", q_latent, cache_latent, preferred_element_type=jnp.float32)
    scores = scores + jnp.einsum(
        "rdh,rdp->rhp", q_rope, cache_rope, preferred_element_type=jnp.float32
    )
    scores = score_scale * scores
    global_pos = lax.axis_index("exp") * positions + jnp.arange(positions, dtype=jnp.int32)
    is_live = global_pos[None, None, :] < lengths[:, None, None]
    masked = jnp.where(is_live, scores, neg_fill)
    block_max = jnp.max(masked, axis=2)
    weights = jnp.where(is_live, jnp.exp(masked - block_max[:, :, None]), 0.0)
    block_sum = jnp.sum(weights, axis=2)
    block_out = jnp.einsum(
        "rhp,rpl->rhl",
        weights.astype(jnp.bfloat16),
        cache_latent,
        preferred_element_type=jnp.float32,
    )
    row_top = lax.pmax(block_max, "exp")
    factor = jnp.exp(block_max - row_top)
    numerator, denominator = (
        lax.psum_scatter(block_out * factor[:, :, None], "exp", scatter_dimension=1, tiled=True),
        lax.psum_scatter(block_sum * factor, "exp", scatter_dimension=1, tiled=True),
    )
    attn_out = (numerator / denominator[:, :, None]).astype(jnp.bfloat16)
    moe_out = routed_experts(tokens, route_ids, route_gates, w_gate, w_up, w_down)
    return (attn_out, moe_out)


def solution(mesh):
    return jax.shard_map(
        per_device,
        mesh=mesh,
        in_specs=(
            P("attn", None, None),
            P("attn", None, None),
            P("attn", "exp", None),
            P("attn", None, "exp"),
            P("attn"),
            P(("attn", "exp"), None),
            P(("attn", "exp"), None),
            P(("attn", "exp"), None),
            P("attn", None, "exp"),
            P("attn", None, "exp"),
            P("attn", "exp", None),
        ),
        out_specs=(P("attn", "exp", None), P(("attn", "exp"), None)),
        check_vma=False,
    )
```

```python
import math

import jax
import jax.numpy as jnp
from jax import lax
from jax.sharding import PartitionSpec as P

score_scale = 1.0 / math.sqrt(192.0)
neg_fill = -1e30


def expert_part(row_block, gate_slice, up_slice, down_slice):
    gate_value = jnp.dot(row_block, gate_slice, preferred_element_type=jnp.float32)
    upward = jnp.dot(row_block, up_slice, preferred_element_type=jnp.float32)
    hidden = (jax.nn.silu(gate_value) * upward).astype(jnp.bfloat16)
    return jnp.dot(hidden, down_slice, preferred_element_type=jnp.float32)


def shift_gather(x, axis, n):
    pieces = [x]
    for k in range(1, n):
        pieces.append(lax.ppermute(x, axis, [(i, (i + k) % n) for i in range(n)]))
    return jnp.stack(pieces)


def shift_scatter_sum(q, axis, n):
    total = q[0]
    for k in range(1, n):
        total = total + lax.ppermute(q[k], axis, [(i, (i - k) % n) for i in range(n)])
    return total


def bit_gather(x, axis, bit, n):
    other = lax.ppermute(x, axis, [(i, i ^ bit) for i in range(n)])
    return jnp.stack([x, other])


def bit_reduce(x, axis, bit, n):
    return x[0] + lax.ppermute(x[1], axis, [(i, i ^ bit) for i in range(n)])


def routed_experts(tokens, route_ids, route_gates, w_gate, w_up, w_down):
    n_exp = lax.axis_size("exp")
    n_attn = lax.axis_size("attn")
    n_local = w_gate.shape[0]
    n_experts = n_attn * n_local
    tok_count, model_width = tokens.shape
    bits = []
    b = n_exp // 2
    while b >= 1:
        bits.append(b)
        b //= 2
    hit = route_ids[:, :, None] == jnp.arange(n_experts, dtype=jnp.int32)[None, None, :]
    wmat = jnp.sum(jnp.where(hit, route_gates[:, :, None], 0.0), axis=1)
    rows = shift_gather(tokens, "attn", n_attn)
    for bit in bits:
        rows = bit_gather(rows, "exp", bit, n_exp)
    lead_shape = rows.shape[:-1]
    flat_rows = rows.reshape(-1, model_width)
    me = lax.axis_index("attn")
    owners = (me + jnp.arange(n_attn, dtype=jnp.int32)) % n_attn
    result = jnp.zeros((tok_count, model_width), jnp.float32)
    for i in range(n_local):
        partial = expert_part(flat_rows, w_gate[i], w_up[i], w_down[i])
        partial = partial.reshape(lead_shape + (model_width,))
        for bit in reversed(bits):
            partial = bit_reduce(partial, "exp", bit, n_exp)
        expert_rows = partial.astype(jnp.bfloat16)
        back = [expert_rows[0]]
        for k in range(1, n_attn):
            back.append(
                lax.ppermute(expert_rows[k], "attn", [(s, (s - k) % n_attn) for s in range(n_attn)])
            )
        chosen = jnp.take(wmat, owners * n_local + i, axis=1)
        for k in range(n_attn):
            result = result + chosen[:, k : k + 1] * back[k].astype(jnp.float32)
    return result.astype(jnp.bfloat16)

def per_device(
    q_latent,
    q_rope,
    cache_latent,
    cache_rope,
    lengths,
    tokens,
    route_ids,
    route_gates,
    w_gate,
    w_up,
    w_down,
):
    n_exp = lax.axis_size("exp")
    n_attn = lax.axis_size("attn")
    positions = cache_latent.shape[1]
    scores = jnp.einsum("rhl,rpl->rhp", q_latent, cache_latent, preferred_element_type=jnp.float32)
    scores = scores + jnp.einsum(
        "rdh,rdp->rhp", q_rope, cache_rope, preferred_element_type=jnp.float32
    )
    scores = score_scale * scores
    global_pos = lax.axis_index("exp") * positions + jnp.arange(positions, dtype=jnp.int32)
    is_live = global_pos[None, None, :] < lengths[:, None, None]
    masked = jnp.where(is_live, scores, neg_fill)
    block_max = jnp.max(masked, axis=2)
    weights = jnp.where(is_live, jnp.exp(masked - block_max[:, :, None]), 0.0)
    block_sum = jnp.sum(weights, axis=2)
    block_out = jnp.einsum(
        "rhp,rpl->rhl",
        weights.astype(jnp.bfloat16),
        cache_latent,
        preferred_element_type=jnp.float32,
    )
    row_top = lax.pmax(block_max, "exp")
    factor = jnp.exp(block_max - row_top)
    numerator, denominator = (
        lax.psum_scatter(block_out * factor[:, :, None], "exp", scatter_dimension=1, tiled=True),
        lax.psum_scatter(block_sum * factor, "exp", scatter_dimension=1, tiled=True),
    )
    attn_out = (numerator / denominator[:, :, None]).astype(jnp.bfloat16)
    moe_out = routed_experts(tokens, route_ids, route_gates, w_gate, w_up, w_down)
    return (attn_out, moe_out)


def solution(mesh):
    return jax.shard_map(
        per_device,
        mesh=mesh,
        in_specs=(
            P("attn", None, None),
            P("attn", None, None),
            P("attn", "exp", None),
            P("attn", None, "exp"),
            P("attn"),
            P(("attn", "exp"), None),
            P(("attn", "exp"), None),
            P(("attn", "exp"), None),
            P("attn", None, "exp"),
            P("attn", None, "exp"),
            P("attn", "exp", None),
        ),
        out_specs=(P("attn", "exp", None), P(("attn", "exp"), None)),
        check_vma=False,
    )
```

```python
import math

import jax
import jax.numpy as jnp
from jax import lax
from jax.sharding import PartitionSpec as P

score_scale = 1.0 / math.sqrt(192.0)
neg_fill = -1e30


def expert_part(row_block, gate_slice, up_slice, down_slice):
    gate_value = jnp.dot(row_block, gate_slice, preferred_element_type=jnp.float32)
    upward = jnp.dot(row_block, up_slice, preferred_element_type=jnp.float32)
    hidden = (jax.nn.silu(gate_value) * upward).astype(jnp.bfloat16)
    return jnp.dot(hidden, down_slice, preferred_element_type=jnp.float32)


def shift_gather(x, axis, n):
    pieces = [x]
    for k in range(1, n):
        pieces.append(lax.ppermute(x, axis, [(i, (i + k) % n) for i in range(n)]))
    return jnp.stack(pieces)


def shift_scatter_sum(q, axis, n):
    total = q[0]
    for k in range(1, n):
        total = total + lax.ppermute(q[k], axis, [(i, (i - k) % n) for i in range(n)])
    return total


def bit_gather(x, axis, bit, n):
    other = lax.ppermute(x, axis, [(i, i ^ bit) for i in range(n)])
    return jnp.stack([x, other])


def bit_reduce(x, axis, bit, n):
    return x[0] + lax.ppermute(x[1], axis, [(i, i ^ bit) for i in range(n)])


def routed_experts(tokens, route_ids, route_gates, w_gate, w_up, w_down, earlier):
    n_exp = lax.axis_size("exp")
    n_attn = lax.axis_size("attn")
    n_local = w_gate.shape[0]
    n_experts = n_attn * n_local
    tok_count, model_width = tokens.shape
    bits = []
    b = n_exp // 2
    while b >= 1:
        bits.append(b)
        b //= 2
    hit = route_ids[:, :, None] == jnp.arange(n_experts, dtype=jnp.int32)[None, None, :]
    wmat = jnp.sum(jnp.where(hit, route_gates[:, :, None], 0.0), axis=1)
    rows = shift_gather(tokens, "attn", n_attn)
    rows, _ = lax.optimization_barrier((rows, earlier))
    for bit in bits:
        rows = bit_gather(rows, "exp", bit, n_exp)
    lead_shape = rows.shape[:-1]
    flat_rows = rows.reshape(-1, model_width)
    me = lax.axis_index("attn")
    owners = (me + jnp.arange(n_attn, dtype=jnp.int32)) % n_attn
    result = jnp.zeros((tok_count, model_width), jnp.float32)
    for i in range(n_local):
        partial = expert_part(flat_rows, w_gate[i], w_up[i], w_down[i])
        partial = partial.reshape(lead_shape + (model_width,))
        for bit in reversed(bits):
            partial = bit_reduce(partial, "exp", bit, n_exp)
        expert_rows = partial.astype(jnp.bfloat16)
        back = [expert_rows[0]]
        for k in range(1, n_attn):
            back.append(
                lax.ppermute(expert_rows[k], "attn", [(s, (s - k) % n_attn) for s in range(n_attn)])
            )
        chosen = jnp.take(wmat, owners * n_local + i, axis=1)
        for k in range(n_attn):
            result = result + chosen[:, k : k + 1] * back[k].astype(jnp.float32)
    return result.astype(jnp.bfloat16)

def per_device(
    q_latent,
    q_rope,
    cache_latent,
    cache_rope,
    lengths,
    tokens,
    route_ids,
    route_gates,
    w_gate,
    w_up,
    w_down,
):
    n_exp = lax.axis_size("exp")
    n_attn = lax.axis_size("attn")
    positions = cache_latent.shape[1]
    scores = jnp.einsum("rhl,rpl->rhp", q_latent, cache_latent, preferred_element_type=jnp.float32)
    scores = scores + jnp.einsum(
        "rdh,rdp->rhp", q_rope, cache_rope, preferred_element_type=jnp.float32
    )
    scores = score_scale * scores
    global_pos = lax.axis_index("exp") * positions + jnp.arange(positions, dtype=jnp.int32)
    is_live = global_pos[None, None, :] < lengths[:, None, None]
    masked = jnp.where(is_live, scores, neg_fill)
    block_max = jnp.max(masked, axis=2)
    weights = jnp.where(is_live, jnp.exp(masked - block_max[:, :, None]), 0.0)
    block_sum = jnp.sum(weights, axis=2)
    block_out = jnp.einsum(
        "rhp,rpl->rhl",
        weights.astype(jnp.bfloat16),
        cache_latent,
        preferred_element_type=jnp.float32,
    )
    row_top = jnp.max(lax.all_gather(block_max, "exp", axis=0), axis=0)
    factor = jnp.exp(block_max - row_top)
    packed = jnp.concatenate([block_out * factor[:, :, None], (block_sum * factor)[:, :, None]], axis=2)
    reduced = lax.psum_scatter(packed, "exp", scatter_dimension=1, tiled=True)
    numerator, denominator = reduced[:, :, :-1], reduced[:, :, -1]
    attn_out = (numerator / denominator[:, :, None]).astype(jnp.bfloat16)
    moe_out = routed_experts(tokens, route_ids, route_gates, w_gate, w_up, w_down, attn_out)
    return (attn_out, moe_out)


def solution(mesh):
    return jax.shard_map(
        per_device,
        mesh=mesh,
        in_specs=(
            P("attn", None, None),
            P("attn", None, None),
            P("attn", "exp", None),
            P("attn", None, "exp"),
            P("attn"),
            P(("attn", "exp"), None),
            P(("attn", "exp"), None),
            P(("attn", "exp"), None),
            P("attn", None, "exp"),
            P("attn", None, "exp"),
            P("attn", "exp", None),
        ),
        out_specs=(P("attn", "exp", None), P(("attn", "exp"), None)),
        check_vma=False,
    )
```

```python
import math

import jax
import jax.numpy as jnp
from jax import lax
from jax.sharding import PartitionSpec as P

score_scale = 1.0 / math.sqrt(192.0)
neg_fill = -1e30


def expert_part(row_block, gate_slice, up_slice, down_slice):
    gate_value = jnp.dot(row_block, gate_slice, preferred_element_type=jnp.float32)
    upward = jnp.dot(row_block, up_slice, preferred_element_type=jnp.float32)
    hidden = (jax.nn.silu(gate_value) * upward).astype(jnp.bfloat16)
    return jnp.dot(hidden, down_slice, preferred_element_type=jnp.float32)


def shift_gather(x, axis, n):
    pieces = [x]
    for k in range(1, n):
        pieces.append(lax.ppermute(x, axis, [(i, (i + k) % n) for i in range(n)]))
    return jnp.stack(pieces)


def shift_scatter_sum(q, axis, n):
    total = q[0]
    for k in range(1, n):
        total = total + lax.ppermute(q[k], axis, [(i, (i - k) % n) for i in range(n)])
    return total


def bit_gather(x, axis, bit, n):
    other = lax.ppermute(x, axis, [(i, i ^ bit) for i in range(n)])
    return jnp.stack([x, other])


def bit_reduce(x, axis, bit, n, wire=None):
    sent = x[1] if wire is None else x[1].astype(wire)
    return x[0] + lax.ppermute(sent, axis, [(i, i ^ bit) for i in range(n)]).astype(x.dtype)


def routed_experts(tokens, route_ids, route_gates, w_gate, w_up, w_down, earlier):
    n_exp = lax.axis_size("exp")
    n_attn = lax.axis_size("attn")
    n_local = w_gate.shape[0]
    n_experts = n_attn * n_local
    tok_count, model_width = tokens.shape
    bits = []
    b = n_exp // 2
    while b >= 1:
        bits.append(b)
        b //= 2
    hit = route_ids[:, :, None] == jnp.arange(n_experts, dtype=jnp.int32)[None, None, :]
    wmat = jnp.sum(jnp.where(hit, route_gates[:, :, None], 0.0), axis=1)
    rows = shift_gather(tokens, "attn", n_attn)
    rows, _ = lax.optimization_barrier((rows, earlier))
    for bit in bits:
        rows = bit_gather(rows, "exp", bit, n_exp)
    lead_shape = rows.shape[:-1]
    flat_rows = rows.reshape(-1, model_width)
    me = lax.axis_index("attn")
    owners = (me + jnp.arange(n_attn, dtype=jnp.int32)) % n_attn
    result = jnp.zeros((tok_count, model_width), jnp.float32)
    for i in range(n_local):
        partial = expert_part(flat_rows, w_gate[i], w_up[i], w_down[i])
        partial = partial.reshape(lead_shape + (model_width,))
        for bit in reversed(bits):
            wire = jnp.bfloat16 if bit == bits[0] else None
            partial = bit_reduce(partial, "exp", bit, n_exp, wire)
        expert_rows = partial.astype(jnp.bfloat16)
        back = [expert_rows[0]]
        for k in range(1, n_attn):
            back.append(
                lax.ppermute(expert_rows[k], "attn", [(s, (s - k) % n_attn) for s in range(n_attn)])
            )
        chosen = jnp.take(wmat, owners * n_local + i, axis=1)
        for k in range(n_attn):
            result = result + chosen[:, k : k + 1] * back[k].astype(jnp.float32)
    return result.astype(jnp.bfloat16)

def per_device(
    q_latent,
    q_rope,
    cache_latent,
    cache_rope,
    lengths,
    tokens,
    route_ids,
    route_gates,
    w_gate,
    w_up,
    w_down,
):
    n_exp = lax.axis_size("exp")
    n_attn = lax.axis_size("attn")
    positions = cache_latent.shape[1]
    scores = jnp.einsum("rhl,rpl->rhp", q_latent, cache_latent, preferred_element_type=jnp.float32)
    scores = scores + jnp.einsum(
        "rdh,rdp->rhp", q_rope, cache_rope, preferred_element_type=jnp.float32
    )
    scores = score_scale * scores
    global_pos = lax.axis_index("exp") * positions + jnp.arange(positions, dtype=jnp.int32)
    is_live = global_pos[None, None, :] < lengths[:, None, None]
    masked = jnp.where(is_live, scores, neg_fill)
    block_max = jnp.max(masked, axis=2)
    weights = jnp.where(is_live, jnp.exp(masked - block_max[:, :, None]), 0.0)
    block_sum = jnp.sum(weights, axis=2)
    block_out = jnp.einsum(
        "rhp,rpl->rhl",
        weights.astype(jnp.bfloat16),
        cache_latent,
        preferred_element_type=jnp.float32,
    )
    row_top = jnp.max(lax.all_gather(block_max, "exp", axis=0), axis=0)
    factor = jnp.exp(block_max - row_top)
    packed = jnp.concatenate([block_out * factor[:, :, None], (block_sum * factor)[:, :, None]], axis=2)
    reduced = lax.psum_scatter(packed, "exp", scatter_dimension=1, tiled=True)
    numerator, denominator = reduced[:, :, :-1], reduced[:, :, -1]
    attn_out = (numerator / denominator[:, :, None]).astype(jnp.bfloat16)
    moe_out = routed_experts(tokens, route_ids, route_gates, w_gate, w_up, w_down, attn_out)
    return (attn_out, moe_out)


def solution(mesh):
    return jax.shard_map(
        per_device,
        mesh=mesh,
        in_specs=(
            P("attn", None, None),
            P("attn", None, None),
            P("attn", "exp", None),
            P("attn", None, "exp"),
            P("attn"),
            P(("attn", "exp"), None),
            P(("attn", "exp"), None),
            P(("attn", "exp"), None),
            P("attn", None, "exp"),
            P("attn", None, "exp"),
            P("attn", "exp", None),
        ),
        out_specs=(P("attn", "exp", None), P(("attn", "exp"), None)),
        check_vma=False,
    )
```

```python
import math

import jax
import jax.numpy as jnp
from jax import lax
from jax.sharding import PartitionSpec as P

score_scale = 1.0 / math.sqrt(192.0)
neg_fill = -1e30


def expert_part(row_block, gate_slice, up_slice, down_slice):
    gate_value = jnp.dot(row_block, gate_slice, preferred_element_type=jnp.float32)
    upward = jnp.dot(row_block, up_slice, preferred_element_type=jnp.float32)
    hidden = (jax.nn.silu(gate_value) * upward).astype(jnp.bfloat16)
    return jnp.dot(hidden, down_slice, preferred_element_type=jnp.float32)


def shift_gather(x, axis, n):
    pieces = [x]
    for k in range(1, n):
        pieces.append(lax.ppermute(x, axis, [(i, (i + k) % n) for i in range(n)]))
    return jnp.stack(pieces)


def shift_scatter_sum(q, axis, n):
    total = q[0]
    for k in range(1, n):
        total = total + lax.ppermute(q[k], axis, [(i, (i - k) % n) for i in range(n)])
    return total


def bit_gather(x, axis, bit, n):
    other = lax.ppermute(x, axis, [(i, i ^ bit) for i in range(n)])
    return jnp.stack([x, other])


def bit_reduce(x, axis, bit, n, wire=None):
    sent = x[1] if wire is None else x[1].astype(wire)
    return x[0] + lax.ppermute(sent, axis, [(i, i ^ bit) for i in range(n)]).astype(x.dtype)


def routed_experts(tokens, route_ids, route_gates, w_gate, w_up, w_down, packed):
    n_exp = lax.axis_size("exp")
    n_attn = lax.axis_size("attn")
    n_local = w_gate.shape[0]
    n_experts = n_attn * n_local
    tok_count, model_width = tokens.shape
    bits = []
    b = n_exp // 2
    while b >= 1:
        bits.append(b)
        b //= 2
    hit = route_ids[:, :, None] == jnp.arange(n_experts, dtype=jnp.int32)[None, None, :]
    wmat = jnp.sum(jnp.where(hit, route_gates[:, :, None], 0.0), axis=1)
    rows = shift_gather(tokens, "attn", n_attn)
    for bit in bits:
        rows = bit_gather(rows, "exp", bit, n_exp)
    rows, packed = lax.optimization_barrier((rows, packed))
    reduced = lax.psum_scatter(packed, "exp", scatter_dimension=1, tiled=True)
    numerator, denominator = reduced[:, :, :-1], reduced[:, :, -1]
    attn_out = (numerator / denominator[:, :, None]).astype(jnp.bfloat16)
    lead_shape = rows.shape[:-1]
    flat_rows = rows.reshape(-1, model_width)
    me = lax.axis_index("attn")
    owners = (me + jnp.arange(n_attn, dtype=jnp.int32)) % n_attn
    result = jnp.zeros((tok_count, model_width), jnp.float32)
    for i in range(n_local):
        partial = expert_part(flat_rows, w_gate[i], w_up[i], w_down[i])
        partial = partial.reshape(lead_shape + (model_width,))
        for bit in reversed(bits):
            if bit == bits[0]:
                partial, attn_out = lax.optimization_barrier((partial, attn_out))
            wire = jnp.bfloat16 if bit == bits[0] else None
            partial = bit_reduce(partial, "exp", bit, n_exp, wire)
        expert_rows = partial.astype(jnp.bfloat16)
        back = [expert_rows[0]]
        for k in range(1, n_attn):
            back.append(
                lax.ppermute(expert_rows[k], "attn", [(s, (s - k) % n_attn) for s in range(n_attn)])
            )
        chosen = jnp.take(wmat, owners * n_local + i, axis=1)
        for k in range(n_attn):
            result = result + chosen[:, k : k + 1] * back[k].astype(jnp.float32)
    return result.astype(jnp.bfloat16), attn_out

def per_device(
    q_latent,
    q_rope,
    cache_latent,
    cache_rope,
    lengths,
    tokens,
    route_ids,
    route_gates,
    w_gate,
    w_up,
    w_down,
):
    n_exp = lax.axis_size("exp")
    n_attn = lax.axis_size("attn")
    positions = cache_latent.shape[1]
    scores = jnp.einsum("rhl,rpl->rhp", q_latent, cache_latent, preferred_element_type=jnp.float32)
    scores = scores + jnp.einsum(
        "rdh,rdp->rhp", q_rope, cache_rope, preferred_element_type=jnp.float32
    )
    scores = score_scale * scores
    global_pos = lax.axis_index("exp") * positions + jnp.arange(positions, dtype=jnp.int32)
    is_live = global_pos[None, None, :] < lengths[:, None, None]
    masked = jnp.where(is_live, scores, neg_fill)
    block_max = jnp.max(masked, axis=2)
    weights = jnp.where(is_live, jnp.exp(masked - block_max[:, :, None]), 0.0)
    block_sum = jnp.sum(weights, axis=2)
    block_out = jnp.einsum(
        "rhp,rpl->rhl",
        weights.astype(jnp.bfloat16),
        cache_latent,
        preferred_element_type=jnp.float32,
    )
    row_top = jnp.max(lax.all_gather(block_max, "exp", axis=0), axis=0)
    factor = jnp.exp(block_max - row_top)
    packed = jnp.concatenate([block_out * factor[:, :, None], (block_sum * factor)[:, :, None]], axis=2)
    moe_out, attn_out = routed_experts(tokens, route_ids, route_gates, w_gate, w_up, w_down, packed)
    return (attn_out, moe_out)


def solution(mesh):
    return jax.shard_map(
        per_device,
        mesh=mesh,
        in_specs=(
            P("attn", None, None),
            P("attn", None, None),
            P("attn", "exp", None),
            P("attn", None, "exp"),
            P("attn"),
            P(("attn", "exp"), None),
            P(("attn", "exp"), None),
            P(("attn", "exp"), None),
            P("attn", None, "exp"),
            P("attn", None, "exp"),
            P("attn", "exp", None),
        ),
        out_specs=(P("attn", "exp", None), P(("attn", "exp"), None)),
        check_vma=False,
    )
```

```python
import math

import jax
import jax.numpy as jnp
from jax import lax
from jax.sharding import PartitionSpec as P

score_scale = 1.0 / math.sqrt(192.0)
neg_fill = -1e30


def expert_part(row_block, gate_slice, up_slice, down_slice):
    gate_value = jnp.dot(row_block, gate_slice, preferred_element_type=jnp.float32)
    upward = jnp.dot(row_block, up_slice, preferred_element_type=jnp.float32)
    hidden = (jax.nn.silu(gate_value) * upward).astype(jnp.bfloat16)
    return jnp.dot(hidden, down_slice, preferred_element_type=jnp.float32)


def shift_gather(x, axis, n):
    pieces = [x]
    for k in range(1, n):
        pieces.append(lax.ppermute(x, axis, [(i, (i + k) % n) for i in range(n)]))
    return jnp.stack(pieces)


def shift_scatter_sum(q, axis, n):
    total = q[0]
    for k in range(1, n):
        total = total + lax.ppermute(q[k], axis, [(i, (i - k) % n) for i in range(n)])
    return total


def bit_gather(x, axis, bit, n):
    other = lax.ppermute(x, axis, [(i, i ^ bit) for i in range(n)])
    return jnp.stack([x, other])


def bit_reduce(x, axis, bit, n, wire=None):
    sent = x[1] if wire is None else x[1].astype(wire)
    return x[0] + lax.ppermute(sent, axis, [(i, i ^ bit) for i in range(n)]).astype(x.dtype)


def routed_experts(tokens, route_ids, route_gates, w_gate, w_up, w_down, earlier):
    n_exp = lax.axis_size("exp")
    n_attn = lax.axis_size("attn")
    n_local = w_gate.shape[0]
    n_experts = n_attn * n_local
    tok_count, model_width = tokens.shape
    bits = []
    b = n_exp // 2
    while b >= 1:
        bits.append(b)
        b //= 2
    hit = route_ids[:, :, None] == jnp.arange(n_experts, dtype=jnp.int32)[None, None, :]
    wmat = jnp.sum(jnp.where(hit, route_gates[:, :, None], 0.0), axis=1)
    n_chunks = 2 if n_attn % 2 == 0 else 1
    per_chunk = n_attn // n_chunks
    pieces = [tokens]
    for k in range(1, n_attn):
        pieces.append(lax.ppermute(tokens, "attn", [(s, (s + k) % n_attn) for s in range(n_attn)]))
    blocks = []
    for c in range(n_chunks):
        block = jnp.stack(pieces[c * per_chunk : (c + 1) * per_chunk])
        if c == 0:
            block, _ = lax.optimization_barrier((block, earlier))
        for bit in bits:
            block = bit_gather(block, "exp", bit, n_exp)
        blocks.append(block)
    rows = jnp.stack(blocks)
    lead_shape = rows.shape[:-1]
    flat_rows = rows.reshape(-1, model_width)
    me = lax.axis_index("attn")
    owners = (me + jnp.arange(n_attn, dtype=jnp.int32)) % n_attn
    result = jnp.zeros((tok_count, model_width), jnp.float32)
    for i in range(n_local):
        partial = expert_part(flat_rows, w_gate[i], w_up[i], w_down[i])
        partial = partial.reshape(lead_shape + (model_width,))
        chosen = jnp.take(wmat, owners * n_local + i, axis=1)
        for c in range(n_chunks):
            part = partial[c]
            for bit in reversed(bits):
                wire = jnp.bfloat16 if bit == bits[0] else None
                part = bit_reduce(part, "exp", bit, n_exp, wire)
            expert_rows = part.astype(jnp.bfloat16)
            for kk in range(per_chunk):
                k = c * per_chunk + kk
                if k == 0:
                    back = expert_rows[kk]
                else:
                    back = lax.ppermute(
                        expert_rows[kk], "attn", [(s, (s - k) % n_attn) for s in range(n_attn)]
                    )
                result = result + chosen[:, k : k + 1] * back.astype(jnp.float32)
    return result.astype(jnp.bfloat16)

def per_device(
    q_latent,
    q_rope,
    cache_latent,
    cache_rope,
    lengths,
    tokens,
    route_ids,
    route_gates,
    w_gate,
    w_up,
    w_down,
):
    n_exp = lax.axis_size("exp")
    n_attn = lax.axis_size("attn")
    positions = cache_latent.shape[1]
    scores = jnp.einsum("rhl,rpl->rhp", q_latent, cache_latent, preferred_element_type=jnp.float32)
    scores = scores + jnp.einsum(
        "rdh,rdp->rhp", q_rope, cache_rope, preferred_element_type=jnp.float32
    )
    scores = score_scale * scores
    global_pos = lax.axis_index("exp") * positions + jnp.arange(positions, dtype=jnp.int32)
    is_live = global_pos[None, None, :] < lengths[:, None, None]
    masked = jnp.where(is_live, scores, neg_fill)
    block_max = jnp.max(masked, axis=2)
    weights = jnp.where(is_live, jnp.exp(masked - block_max[:, :, None]), 0.0)
    block_sum = jnp.sum(weights, axis=2)
    block_out = jnp.einsum(
        "rhp,rpl->rhl",
        weights.astype(jnp.bfloat16),
        cache_latent,
        preferred_element_type=jnp.float32,
    )
    row_top = jnp.max(lax.all_gather(block_max, "exp", axis=0), axis=0)
    factor = jnp.exp(block_max - row_top)
    packed = jnp.concatenate([block_out * factor[:, :, None], (block_sum * factor)[:, :, None]], axis=2)
    reduced = lax.psum_scatter(packed, "exp", scatter_dimension=1, tiled=True)
    numerator, denominator = reduced[:, :, :-1], reduced[:, :, -1]
    attn_out = (numerator / denominator[:, :, None]).astype(jnp.bfloat16)
    moe_out = routed_experts(tokens, route_ids, route_gates, w_gate, w_up, w_down, attn_out)
    return (attn_out, moe_out)


def solution(mesh):
    return jax.shard_map(
        per_device,
        mesh=mesh,
        in_specs=(
            P("attn", None, None),
            P("attn", None, None),
            P("attn", "exp", None),
            P("attn", None, "exp"),
            P("attn"),
            P(("attn", "exp"), None),
            P(("attn", "exp"), None),
            P(("attn", "exp"), None),
            P("attn", None, "exp"),
            P("attn", None, "exp"),
            P("attn", "exp", None),
        ),
        out_specs=(P("attn", "exp", None), P(("attn", "exp"), None)),
        check_vma=False,
    )
```

```python
import math

import jax
import jax.numpy as jnp
from jax import lax
from jax.sharding import PartitionSpec as P

score_scale = 1.0 / math.sqrt(192.0)
neg_fill = -1e30


def expert_part(row_block, gate_slice, up_slice, down_slice):
    gate_value = jnp.dot(row_block, gate_slice, preferred_element_type=jnp.float32)
    upward = jnp.dot(row_block, up_slice, preferred_element_type=jnp.float32)
    hidden = (jax.nn.silu(gate_value) * upward).astype(jnp.bfloat16)
    return jnp.dot(hidden, down_slice, preferred_element_type=jnp.float32)


def shift_gather(x, axis, n):
    pieces = [x]
    for k in range(1, n):
        pieces.append(lax.ppermute(x, axis, [(i, (i + k) % n) for i in range(n)]))
    return jnp.stack(pieces)


def shift_scatter_sum(q, axis, n):
    total = q[0]
    for k in range(1, n):
        total = total + lax.ppermute(q[k], axis, [(i, (i - k) % n) for i in range(n)])
    return total


def bit_gather(x, axis, bit, n):
    other = lax.ppermute(x, axis, [(i, i ^ bit) for i in range(n)])
    return jnp.stack([x, other])


def bit_reduce(x, axis, bit, n, wire=None):
    sent = x[1] if wire is None else x[1].astype(wire)
    return x[0] + lax.ppermute(sent, axis, [(i, i ^ bit) for i in range(n)]).astype(x.dtype)


def routed_experts(tokens, route_ids, route_gates, w_gate, w_up, w_down, earlier):
    n_exp = lax.axis_size("exp")
    n_attn = lax.axis_size("attn")
    n_local = w_gate.shape[0]
    n_experts = n_attn * n_local
    tok_count, model_width = tokens.shape
    bits = []
    b = n_exp // 2
    while b >= 1:
        bits.append(b)
        b //= 2
    hit = route_ids[:, :, None] == jnp.arange(n_experts, dtype=jnp.int32)[None, None, :]
    wmat = jnp.sum(jnp.where(hit, route_gates[:, :, None], 0.0), axis=1)
    n_chunks = 2 if n_attn % 2 == 0 else 1
    per_chunk = n_attn // n_chunks
    pieces = [tokens]
    for k in range(1, n_attn):
        pieces.append(lax.ppermute(tokens, "attn", [(s, (s + k) % n_attn) for s in range(n_attn)]))
    blocks = []
    for c in range(n_chunks):
        block = jnp.stack(pieces[c * per_chunk : (c + 1) * per_chunk])
        if c == 0:
            block, _ = lax.optimization_barrier((block, earlier))
        for bit in bits:
            block = bit_gather(block, "exp", bit, n_exp)
        blocks.append(block)
    me = lax.axis_index("attn")
    owners = (me + jnp.arange(n_attn, dtype=jnp.int32)) % n_attn
    result = jnp.zeros((tok_count, model_width), jnp.float32)
    for i in range(n_local):
        chosen = jnp.take(wmat, owners * n_local + i, axis=1)
        for c in range(n_chunks):
            block = blocks[c]
            part = expert_part(block.reshape(-1, model_width), w_gate[i], w_up[i], w_down[i])
            part = part.reshape(block.shape[:-1] + (model_width,))
            for bit in reversed(bits):
                wire = jnp.bfloat16 if bit == bits[0] else None
                part = bit_reduce(part, "exp", bit, n_exp, wire)
            expert_rows = part.astype(jnp.bfloat16)
            for kk in range(per_chunk):
                k = c * per_chunk + kk
                if k == 0:
                    back = expert_rows[kk]
                else:
                    back = lax.ppermute(
                        expert_rows[kk], "attn", [(s, (s - k) % n_attn) for s in range(n_attn)]
                    )
                result = result + chosen[:, k : k + 1] * back.astype(jnp.float32)
    return result.astype(jnp.bfloat16)

def per_device(
    q_latent,
    q_rope,
    cache_latent,
    cache_rope,
    lengths,
    tokens,
    route_ids,
    route_gates,
    w_gate,
    w_up,
    w_down,
):
    n_exp = lax.axis_size("exp")
    n_attn = lax.axis_size("attn")
    positions = cache_latent.shape[1]
    scores = jnp.einsum("rhl,rpl->rhp", q_latent, cache_latent, preferred_element_type=jnp.float32)
    scores = scores + jnp.einsum(
        "rdh,rdp->rhp", q_rope, cache_rope, preferred_element_type=jnp.float32
    )
    scores = score_scale * scores
    global_pos = lax.axis_index("exp") * positions + jnp.arange(positions, dtype=jnp.int32)
    is_live = global_pos[None, None, :] < lengths[:, None, None]
    masked = jnp.where(is_live, scores, neg_fill)
    block_max = jnp.max(masked, axis=2)
    weights = jnp.where(is_live, jnp.exp(masked - block_max[:, :, None]), 0.0)
    block_sum = jnp.sum(weights, axis=2)
    block_out = jnp.einsum(
        "rhp,rpl->rhl",
        weights.astype(jnp.bfloat16),
        cache_latent,
        preferred_element_type=jnp.float32,
    )
    row_top = jnp.max(lax.all_gather(block_max, "exp", axis=0), axis=0)
    factor = jnp.exp(block_max - row_top)
    packed = jnp.concatenate([block_out * factor[:, :, None], (block_sum * factor)[:, :, None]], axis=2)
    reduced = lax.psum_scatter(packed, "exp", scatter_dimension=1, tiled=True)
    numerator, denominator = reduced[:, :, :-1], reduced[:, :, -1]
    attn_out = (numerator / denominator[:, :, None]).astype(jnp.bfloat16)
    moe_out = routed_experts(tokens, route_ids, route_gates, w_gate, w_up, w_down, attn_out)
    return (attn_out, moe_out)


def solution(mesh):
    return jax.shard_map(
        per_device,
        mesh=mesh,
        in_specs=(
            P("attn", None, None),
            P("attn", None, None),
            P("attn", "exp", None),
            P("attn", None, "exp"),
            P("attn"),
            P(("attn", "exp"), None),
            P(("attn", "exp"), None),
            P(("attn", "exp"), None),
            P("attn", None, "exp"),
            P("attn", None, "exp"),
            P("attn", "exp", None),
        ),
        out_specs=(P("attn", "exp", None), P(("attn", "exp"), None)),
        check_vma=False,
    )
```

```python
import math

import jax
import jax.numpy as jnp
from jax import lax
from jax.sharding import PartitionSpec as P

score_scale = 1.0 / math.sqrt(192.0)
neg_fill = -1e30


def expert_part(row_block, gate_slice, up_slice, down_slice):
    gate_value = jnp.dot(row_block, gate_slice, preferred_element_type=jnp.float32)
    upward = jnp.dot(row_block, up_slice, preferred_element_type=jnp.float32)
    hidden = (jax.nn.silu(gate_value) * upward).astype(jnp.bfloat16)
    return jnp.dot(hidden, down_slice, preferred_element_type=jnp.float32)


def shift_gather(x, axis, n):
    pieces = [x]
    for k in range(1, n):
        pieces.append(lax.ppermute(x, axis, [(i, (i + k) % n) for i in range(n)]))
    return jnp.stack(pieces)


def shift_scatter_sum(q, axis, n):
    total = q[0]
    for k in range(1, n):
        total = total + lax.ppermute(q[k], axis, [(i, (i - k) % n) for i in range(n)])
    return total


def bit_gather(x, axis, bit, n):
    other = lax.ppermute(x, axis, [(i, i ^ bit) for i in range(n)])
    return jnp.stack([x, other])


def bit_reduce(x, axis, bit, n, wire=None):
    sent = x[1] if wire is None else x[1].astype(wire)
    return x[0] + lax.ppermute(sent, axis, [(i, i ^ bit) for i in range(n)]).astype(x.dtype)


def routed_experts(tokens, route_ids, route_gates, w_gate, w_up, w_down, earlier):
    n_exp = lax.axis_size("exp")
    n_attn = lax.axis_size("attn")
    n_local = w_gate.shape[0]
    n_experts = n_attn * n_local
    tok_count, model_width = tokens.shape
    bits = []
    b = n_exp // 2
    while b >= 1:
        bits.append(b)
        b //= 2
    hit = route_ids[:, :, None] == jnp.arange(n_experts, dtype=jnp.int32)[None, None, :]
    wmat = jnp.sum(jnp.where(hit, route_gates[:, :, None], 0.0), axis=1)
    n_chunks = 2 if n_attn % 2 == 0 else 1
    per_chunk = n_attn // n_chunks
    pieces = [tokens]
    for k in range(1, n_attn):
        pieces.append(lax.ppermute(tokens, "attn", [(s, (s + k) % n_attn) for s in range(n_attn)]))
    blocks = []
    for c in range(n_chunks):
        block = jnp.stack(pieces[c * per_chunk : (c + 1) * per_chunk])
        if c == 0:
            block, _ = lax.optimization_barrier((block, earlier))
        for bit in bits:
            block = bit_gather(block, "exp", bit, n_exp)
        blocks.append(block)
    me = lax.axis_index("attn")
    owners = (me + jnp.arange(n_attn, dtype=jnp.int32)) % n_attn
    result = jnp.zeros((tok_count, model_width), jnp.float32)
    for i in range(n_local):
        chosen = jnp.take(wmat, owners * n_local + i, axis=1)
        for c in range(n_chunks):
            block = blocks[c]
            part = expert_part(block.reshape(-1, model_width), w_gate[i], w_up[i], w_down[i])
            part = part.reshape(block.shape[:-1] + (model_width,))
            for bit in reversed(bits):
                wire = jnp.bfloat16 if bit == bits[0] else None
                part = bit_reduce(part, "exp", bit, n_exp, wire)
            expert_rows = part.astype(jnp.bfloat16)
            for kk in range(per_chunk):
                k = c * per_chunk + kk
                if k == 0:
                    back = expert_rows[kk]
                else:
                    back = lax.ppermute(
                        expert_rows[kk], "attn", [(s, (s - k) % n_attn) for s in range(n_attn)]
                    )
                result = result + chosen[:, k : k + 1] * back.astype(jnp.float32)
    return result.astype(jnp.bfloat16)

def per_device(
    q_latent,
    q_rope,
    cache_latent,
    cache_rope,
    lengths,
    tokens,
    route_ids,
    route_gates,
    w_gate,
    w_up,
    w_down,
):
    n_exp = lax.axis_size("exp")
    n_attn = lax.axis_size("attn")
    positions = cache_latent.shape[1]
    scores = jnp.einsum("rhl,rpl->rhp", q_latent, cache_latent, preferred_element_type=jnp.float32)
    scores = scores + jnp.einsum(
        "rdh,rdp->rhp", q_rope, cache_rope, preferred_element_type=jnp.float32
    )
    scores = score_scale * scores
    global_pos = lax.axis_index("exp") * positions + jnp.arange(positions, dtype=jnp.int32)
    is_live = global_pos[None, None, :] < lengths[:, None, None]
    masked = jnp.where(is_live, scores, neg_fill)
    block_max = jnp.max(masked, axis=2)
    weights = jnp.where(is_live, jnp.exp(masked - block_max[:, :, None]), 0.0)
    block_sum = jnp.sum(weights, axis=2)
    block_out = jnp.einsum(
        "rhp,rpl->rhl",
        weights.astype(jnp.bfloat16),
        cache_latent,
        preferred_element_type=jnp.float32,
    )
    me_exp = lax.axis_index("exp")
    row_top = block_max
    bit = 1
    while bit < n_exp:
        row_top = jnp.maximum(
            row_top, lax.ppermute(row_top, "exp", [(i, i ^ bit) for i in range(n_exp)])
        )
        bit *= 2
    factor = jnp.exp(block_max - row_top)
    reduced = jnp.concatenate([block_out * factor[:, :, None], (block_sum * factor)[:, :, None]], axis=2)
    rows_n, heads_n, width = reduced.shape
    bit = 1
    while bit < n_exp:
        outer = n_exp // (2 * bit)
        view = reduced.reshape(rows_n, outer, 2, -1, width)
        mine = (me_exp // bit) % 2
        keep = lax.dynamic_index_in_dim(view, mine, axis=2, keepdims=False)
        sent = lax.dynamic_index_in_dim(view, 1 - mine, axis=2, keepdims=False)
        got = lax.ppermute(sent, "exp", [(i, i ^ bit) for i in range(n_exp)])
        reduced = (keep + got).reshape(rows_n, -1, width)
        bit *= 2
    numerator, denominator = reduced[:, :, :-1], reduced[:, :, -1]
    attn_out = (numerator / denominator[:, :, None]).astype(jnp.bfloat16)
    moe_out = routed_experts(tokens, route_ids, route_gates, w_gate, w_up, w_down, attn_out)
    return (attn_out, moe_out)


def solution(mesh):
    return jax.shard_map(
        per_device,
        mesh=mesh,
        in_specs=(
            P("attn", None, None),
            P("attn", None, None),
            P("attn", "exp", None),
            P("attn", None, "exp"),
            P("attn"),
            P(("attn", "exp"), None),
            P(("attn", "exp"), None),
            P(("attn", "exp"), None),
            P("attn", None, "exp"),
            P("attn", None, "exp"),
            P("attn", "exp", None),
        ),
        out_specs=(P("attn", "exp", None), P(("attn", "exp"), None)),
        check_vma=False,
    )
```

```python
import math

import jax
import jax.numpy as jnp
from jax import lax
from jax.sharding import PartitionSpec as P

score_scale = 1.0 / math.sqrt(192.0)
neg_fill = -1e30


def expert_part(row_block, gate_slice, up_slice, down_slice):
    gate_value = jnp.dot(row_block, gate_slice, preferred_element_type=jnp.float32)
    upward = jnp.dot(row_block, up_slice, preferred_element_type=jnp.float32)
    hidden = (jax.nn.silu(gate_value) * upward).astype(jnp.bfloat16)
    return jnp.dot(hidden, down_slice, preferred_element_type=jnp.float32)


def shift_gather(x, axis, n):
    pieces = [x]
    for k in range(1, n):
        pieces.append(lax.ppermute(x, axis, [(i, (i + k) % n) for i in range(n)]))
    return jnp.stack(pieces)


def shift_scatter_sum(q, axis, n):
    total = q[0]
    for k in range(1, n):
        total = total + lax.ppermute(q[k], axis, [(i, (i - k) % n) for i in range(n)])
    return total


def bit_gather(x, axis, bit, n):
    other = lax.ppermute(x, axis, [(i, i ^ bit) for i in range(n)])
    return jnp.stack([x, other])


def bit_reduce(x, axis, bit, n, wire=None):
    sent = x[1] if wire is None else x[1].astype(wire)
    return x[0] + lax.ppermute(sent, axis, [(i, i ^ bit) for i in range(n)]).astype(x.dtype)


def routed_experts(tokens, route_ids, route_gates, w_gate, w_up, w_down, earlier):
    n_exp = lax.axis_size("exp")
    n_attn = lax.axis_size("attn")
    n_local = w_gate.shape[0]
    n_experts = n_attn * n_local
    tok_count, model_width = tokens.shape
    bits = []
    b = n_exp // 2
    while b >= 1:
        bits.append(b)
        b //= 2
    hit = route_ids[:, :, None] == jnp.arange(n_experts, dtype=jnp.int32)[None, None, :]
    wmat = jnp.sum(jnp.where(hit, route_gates[:, :, None], 0.0), axis=1)
    n_chunks = 2 if n_attn % 2 == 0 else 1
    per_chunk = n_attn // n_chunks
    pieces = [tokens]
    for k in range(1, n_attn):
        pieces.append(lax.ppermute(tokens, "attn", [(s, (s + k) % n_attn) for s in range(n_attn)]))
    blocks = []
    for c in range(n_chunks):
        block = jnp.stack(pieces[c * per_chunk : (c + 1) * per_chunk])
        if c == 0:
            block, _ = lax.optimization_barrier((block, earlier))
        for bit in bits:
            block = bit_gather(block, "exp", bit, n_exp)
        blocks.append(block)
    me = lax.axis_index("attn")
    owners = (me + jnp.arange(n_attn, dtype=jnp.int32)) % n_attn
    result = jnp.zeros((tok_count, model_width), jnp.float32)
    for i in range(n_local):
        chosen = jnp.take(wmat, owners * n_local + i, axis=1)
        halved = [None] * n_chunks
        for c in range(n_chunks):
            block = blocks[c]
            part = expert_part(block.reshape(-1, model_width), w_gate[i], w_up[i], w_down[i])
            part = part.reshape(block.shape[:-1] + (model_width,))
            if c > 0:
                halved[c - 1], part = lax.optimization_barrier((halved[c - 1], part))
            for bit in reversed(bits[1:]):
                part = bit_reduce(part, "exp", bit, n_exp)
            if c + 1 < n_chunks:
                part, blocks[c + 1] = lax.optimization_barrier((part, blocks[c + 1]))
            if bits:
                part = bit_reduce(part, "exp", bits[0], n_exp, jnp.bfloat16)
            halved[c] = part
        for c in range(n_chunks):
            expert_rows = halved[c].astype(jnp.bfloat16)
            for kk in range(per_chunk):
                k = c * per_chunk + kk
                if k == 0:
                    back = expert_rows[kk]
                else:
                    back = lax.ppermute(
                        expert_rows[kk], "attn", [(s, (s - k) % n_attn) for s in range(n_attn)]
                    )
                result = result + chosen[:, k : k + 1] * back.astype(jnp.float32)
    return result.astype(jnp.bfloat16)

def per_device(
    q_latent,
    q_rope,
    cache_latent,
    cache_rope,
    lengths,
    tokens,
    route_ids,
    route_gates,
    w_gate,
    w_up,
    w_down,
):
    n_exp = lax.axis_size("exp")
    n_attn = lax.axis_size("attn")
    positions = cache_latent.shape[1]
    scores = jnp.einsum("rhl,rpl->rhp", q_latent, cache_latent, preferred_element_type=jnp.float32)
    scores = scores + jnp.einsum(
        "rdh,rdp->rhp", q_rope, cache_rope, preferred_element_type=jnp.float32
    )
    scores = score_scale * scores
    global_pos = lax.axis_index("exp") * positions + jnp.arange(positions, dtype=jnp.int32)
    is_live = global_pos[None, None, :] < lengths[:, None, None]
    masked = jnp.where(is_live, scores, neg_fill)
    block_max = jnp.max(masked, axis=2)
    weights = jnp.where(is_live, jnp.exp(masked - block_max[:, :, None]), 0.0)
    block_sum = jnp.sum(weights, axis=2)
    block_out = jnp.einsum(
        "rhp,rpl->rhl",
        weights.astype(jnp.bfloat16),
        cache_latent,
        preferred_element_type=jnp.float32,
    )
    me_exp = lax.axis_index("exp")
    row_top = block_max
    bit = 1
    while bit < n_exp:
        row_top = jnp.maximum(
            row_top, lax.ppermute(row_top, "exp", [(i, i ^ bit) for i in range(n_exp)])
        )
        bit *= 2
    factor = jnp.exp(block_max - row_top)
    reduced = jnp.concatenate([block_out * factor[:, :, None], (block_sum * factor)[:, :, None]], axis=2)
    rows_n, heads_n, width = reduced.shape
    bit = 1
    while bit < n_exp:
        outer = n_exp // (2 * bit)
        view = reduced.reshape(rows_n, outer, 2, -1, width)
        mine = (me_exp // bit) % 2
        keep = lax.dynamic_index_in_dim(view, mine, axis=2, keepdims=False)
        sent = lax.dynamic_index_in_dim(view, 1 - mine, axis=2, keepdims=False)
        got = lax.ppermute(sent, "exp", [(i, i ^ bit) for i in range(n_exp)])
        reduced = (keep + got).reshape(rows_n, -1, width)
        bit *= 2
    numerator, denominator = reduced[:, :, :-1], reduced[:, :, -1]
    attn_out = (numerator / denominator[:, :, None]).astype(jnp.bfloat16)
    moe_out = routed_experts(tokens, route_ids, route_gates, w_gate, w_up, w_down, attn_out)
    return (attn_out, moe_out)


def solution(mesh):
    return jax.shard_map(
        per_device,
        mesh=mesh,
        in_specs=(
            P("attn", None, None),
            P("attn", None, None),
            P("attn", "exp", None),
            P("attn", None, "exp"),
            P("attn"),
            P(("attn", "exp"), None),
            P(("attn", "exp"), None),
            P(("attn", "exp"), None),
            P("attn", None, "exp"),
            P("attn", None, "exp"),
            P("attn", "exp", None),
        ),
        out_specs=(P("attn", "exp", None), P(("attn", "exp"), None)),
        check_vma=False,
    )
```

```python
import math

import jax
import jax.numpy as jnp
from jax import lax
from jax.sharding import PartitionSpec as P

score_scale = 1.0 / math.sqrt(192.0)
neg_fill = -1e30


def expert_part(row_block, gate_slice, up_slice, down_slice):
    gate_value = jnp.dot(row_block, gate_slice, preferred_element_type=jnp.float32)
    upward = jnp.dot(row_block, up_slice, preferred_element_type=jnp.float32)
    hidden = (jax.nn.silu(gate_value) * upward).astype(jnp.bfloat16)
    return jnp.dot(hidden, down_slice, preferred_element_type=jnp.float32)


def shift_gather(x, axis, n):
    pieces = [x]
    for k in range(1, n):
        pieces.append(lax.ppermute(x, axis, [(i, (i + k) % n) for i in range(n)]))
    return jnp.stack(pieces)


def shift_scatter_sum(q, axis, n):
    total = q[0]
    for k in range(1, n):
        total = total + lax.ppermute(q[k], axis, [(i, (i - k) % n) for i in range(n)])
    return total


def bit_gather(x, axis, bit, n):
    other = lax.ppermute(x, axis, [(i, i ^ bit) for i in range(n)])
    return jnp.stack([x, other])


def bit_reduce(x, axis, bit, n, wire=None):
    sent = x[1] if wire is None else x[1].astype(wire)
    return x[0] + lax.ppermute(sent, axis, [(i, i ^ bit) for i in range(n)]).astype(x.dtype)


def routed_experts(tokens, route_ids, route_gates, w_gate, w_up, w_down, earlier):
    n_exp = lax.axis_size("exp")
    n_attn = lax.axis_size("attn")
    n_local = w_gate.shape[0]
    n_experts = n_attn * n_local
    tok_count, model_width = tokens.shape
    bits = []
    b = n_exp // 2
    while b >= 1:
        bits.append(b)
        b //= 2
    hit = route_ids[:, :, None] == jnp.arange(n_experts, dtype=jnp.int32)[None, None, :]
    wmat = jnp.sum(jnp.where(hit, route_gates[:, :, None], 0.0), axis=1)
    n_chunks = 2 if n_attn % 2 == 0 else 1
    per_chunk = n_attn // n_chunks
    pieces = [tokens]
    for k in range(1, n_attn):
        pieces.append(lax.ppermute(tokens, "attn", [(s, (s + k) % n_attn) for s in range(n_attn)]))
    blocks = []
    for c in range(n_chunks):
        block = jnp.stack(pieces[c * per_chunk : (c + 1) * per_chunk])
        for bit in bits:
            block = bit_gather(block, "exp", bit, n_exp)
        blocks.append(block)
    me = lax.axis_index("attn")
    owners = (me + jnp.arange(n_attn, dtype=jnp.int32)) % n_attn
    result = jnp.zeros((tok_count, model_width), jnp.float32)
    for i in range(n_local):
        chosen = jnp.take(wmat, owners * n_local + i, axis=1)
        for c in range(n_chunks):
            block = blocks[c]
            part = expert_part(block.reshape(-1, model_width), w_gate[i], w_up[i], w_down[i])
            part = part.reshape(block.shape[:-1] + (model_width,))
            for bit in reversed(bits):
                wire = jnp.bfloat16 if bit == bits[0] else None
                part = bit_reduce(part, "exp", bit, n_exp, wire)
            expert_rows = part.astype(jnp.bfloat16)
            for kk in range(per_chunk):
                k = c * per_chunk + kk
                if k == 0:
                    back = expert_rows[kk]
                else:
                    back = lax.ppermute(
                        expert_rows[kk], "attn", [(s, (s - k) % n_attn) for s in range(n_attn)]
                    )
                result = result + chosen[:, k : k + 1] * back.astype(jnp.float32)
    return result.astype(jnp.bfloat16)

def per_device(
    q_latent,
    q_rope,
    cache_latent,
    cache_rope,
    lengths,
    tokens,
    route_ids,
    route_gates,
    w_gate,
    w_up,
    w_down,
):
    n_exp = lax.axis_size("exp")
    n_attn = lax.axis_size("attn")
    positions = cache_latent.shape[1]
    scores = jnp.einsum("rhl,rpl->rhp", q_latent, cache_latent, preferred_element_type=jnp.float32)
    scores = scores + jnp.einsum(
        "rdh,rdp->rhp", q_rope, cache_rope, preferred_element_type=jnp.float32
    )
    scores = score_scale * scores
    global_pos = lax.axis_index("exp") * positions + jnp.arange(positions, dtype=jnp.int32)
    is_live = global_pos[None, None, :] < lengths[:, None, None]
    masked = jnp.where(is_live, scores, neg_fill)
    block_max = jnp.max(masked, axis=2)
    weights = jnp.where(is_live, jnp.exp(masked - block_max[:, :, None]), 0.0)
    block_sum = jnp.sum(weights, axis=2)
    block_out = jnp.einsum(
        "rhp,rpl->rhl",
        weights.astype(jnp.bfloat16),
        cache_latent,
        preferred_element_type=jnp.float32,
    )
    me_exp = lax.axis_index("exp")
    row_top = block_max
    bit = 1
    while bit < n_exp:
        row_top = jnp.maximum(
            row_top, lax.ppermute(row_top, "exp", [(i, i ^ bit) for i in range(n_exp)])
        )
        bit *= 2
    factor = jnp.exp(block_max - row_top)
    reduced = jnp.concatenate([block_out * factor[:, :, None], (block_sum * factor)[:, :, None]], axis=2)
    rows_n, heads_n, width = reduced.shape
    bit = 1
    while bit < n_exp:
        outer = n_exp // (2 * bit)
        view = reduced.reshape(rows_n, outer, 2, -1, width)
        mine = (me_exp // bit) % 2
        keep = lax.dynamic_index_in_dim(view, mine, axis=2, keepdims=False)
        sent = lax.dynamic_index_in_dim(view, 1 - mine, axis=2, keepdims=False)
        got = lax.ppermute(sent, "exp", [(i, i ^ bit) for i in range(n_exp)])
        reduced = (keep + got).reshape(rows_n, -1, width)
        bit *= 2
    numerator, denominator = reduced[:, :, :-1], reduced[:, :, -1]
    attn_out = (numerator / denominator[:, :, None]).astype(jnp.bfloat16)
    moe_out = routed_experts(tokens, route_ids, route_gates, w_gate, w_up, w_down, attn_out)
    return (attn_out, moe_out)


def solution(mesh):
    return jax.shard_map(
        per_device,
        mesh=mesh,
        in_specs=(
            P("attn", None, None),
            P("attn", None, None),
            P("attn", "exp", None),
            P("attn", None, "exp"),
            P("attn"),
            P(("attn", "exp"), None),
            P(("attn", "exp"), None),
            P(("attn", "exp"), None),
            P("attn", None, "exp"),
            P("attn", None, "exp"),
            P("attn", "exp", None),
        ),
        out_specs=(P("attn", "exp", None), P(("attn", "exp"), None)),
        check_vma=False,
    )
```

```python
import math

import jax
import jax.numpy as jnp
from jax import lax
from jax.sharding import PartitionSpec as P

score_scale = 1.0 / math.sqrt(192.0)
neg_fill = -1e30


def expert_part(row_block, gate_slice, up_slice, down_slice):
    gate_value = jnp.dot(row_block, gate_slice, preferred_element_type=jnp.float32)
    upward = jnp.dot(row_block, up_slice, preferred_element_type=jnp.float32)
    hidden = (jax.nn.silu(gate_value) * upward).astype(jnp.bfloat16)
    return jnp.dot(hidden, down_slice, preferred_element_type=jnp.float32)


def shift_gather(x, axis, n):
    pieces = [x]
    for k in range(1, n):
        pieces.append(lax.ppermute(x, axis, [(i, (i + k) % n) for i in range(n)]))
    return jnp.stack(pieces)


def shift_scatter_sum(q, axis, n):
    total = q[0]
    for k in range(1, n):
        total = total + lax.ppermute(q[k], axis, [(i, (i - k) % n) for i in range(n)])
    return total


def bit_gather(x, axis, bit, n):
    other = lax.ppermute(x, axis, [(i, i ^ bit) for i in range(n)])
    return jnp.stack([x, other])


def bit_reduce(x, axis, bit, n, wire=None):
    sent = x[1] if wire is None else x[1].astype(wire)
    return x[0] + lax.ppermute(sent, axis, [(i, i ^ bit) for i in range(n)]).astype(x.dtype)


def routed_experts(tokens, route_ids, route_gates, w_gate, w_up, w_down, earlier):
    n_exp = lax.axis_size("exp")
    n_attn = lax.axis_size("attn")
    n_local = w_gate.shape[0]
    n_experts = n_attn * n_local
    tok_count, model_width = tokens.shape
    bits = []
    b = n_exp // 2
    while b >= 1:
        bits.append(b)
        b //= 2
    hit = route_ids[:, :, None] == jnp.arange(n_experts, dtype=jnp.int32)[None, None, :]
    wmat = jnp.sum(jnp.where(hit, route_gates[:, :, None], 0.0), axis=1)
    n_chunks = min(3, n_attn)
    step = -(-n_attn // n_chunks)
    bounds = [min(c * step, n_attn) for c in range(n_chunks)] + [n_attn]
    pieces = [tokens]
    for k in range(1, n_attn):
        pieces.append(lax.ppermute(tokens, "attn", [(s, (s + k) % n_attn) for s in range(n_attn)]))
    blocks = []
    for c in range(n_chunks):
        block = jnp.stack(pieces[bounds[c] : bounds[c + 1]])
        for bit in bits:
            block = bit_gather(block, "exp", bit, n_exp)
        blocks.append(block)
    me = lax.axis_index("attn")
    owners = (me + jnp.arange(n_attn, dtype=jnp.int32)) % n_attn
    result = jnp.zeros((tok_count, model_width), jnp.float32)
    for i in range(n_local):
        chosen = jnp.take(wmat, owners * n_local + i, axis=1)
        for c in range(n_chunks):
            block = blocks[c]
            part = expert_part(block.reshape(-1, model_width), w_gate[i], w_up[i], w_down[i])
            part = part.reshape(block.shape[:-1] + (model_width,))
            for bit in reversed(bits):
                wire = jnp.bfloat16 if bit == bits[0] else None
                part = bit_reduce(part, "exp", bit, n_exp, wire)
            expert_rows = part.astype(jnp.bfloat16)
            for kk in range(bounds[c + 1] - bounds[c]):
                k = bounds[c] + kk
                if k == 0:
                    back = expert_rows[kk]
                else:
                    back = lax.ppermute(
                        expert_rows[kk], "attn", [(s, (s - k) % n_attn) for s in range(n_attn)]
                    )
                result = result + chosen[:, k : k + 1] * back.astype(jnp.float32)
    return result.astype(jnp.bfloat16)

def per_device(
    q_latent,
    q_rope,
    cache_latent,
    cache_rope,
    lengths,
    tokens,
    route_ids,
    route_gates,
    w_gate,
    w_up,
    w_down,
):
    n_exp = lax.axis_size("exp")
    n_attn = lax.axis_size("attn")
    positions = cache_latent.shape[1]
    scores = jnp.einsum("rhl,rpl->rhp", q_latent, cache_latent, preferred_element_type=jnp.float32)
    scores = scores + jnp.einsum(
        "rdh,rdp->rhp", q_rope, cache_rope, preferred_element_type=jnp.float32
    )
    scores = score_scale * scores
    global_pos = lax.axis_index("exp") * positions + jnp.arange(positions, dtype=jnp.int32)
    is_live = global_pos[None, None, :] < lengths[:, None, None]
    masked = jnp.where(is_live, scores, neg_fill)
    block_max = jnp.max(masked, axis=2)
    weights = jnp.where(is_live, jnp.exp(masked - block_max[:, :, None]), 0.0)
    block_sum = jnp.sum(weights, axis=2)
    block_out = jnp.einsum(
        "rhp,rpl->rhl",
        weights.astype(jnp.bfloat16),
        cache_latent,
        preferred_element_type=jnp.float32,
    )
    me_exp = lax.axis_index("exp")
    row_top = block_max
    bit = 1
    while bit < n_exp:
        row_top = jnp.maximum(
            row_top, lax.ppermute(row_top, "exp", [(i, i ^ bit) for i in range(n_exp)])
        )
        bit *= 2
    factor = jnp.exp(block_max - row_top)
    reduced = jnp.concatenate([block_out * factor[:, :, None], (block_sum * factor)[:, :, None]], axis=2)
    rows_n, heads_n, width = reduced.shape
    bit = 1
    while bit < n_exp:
        outer = n_exp // (2 * bit)
        view = reduced.reshape(rows_n, outer, 2, -1, width)
        mine = (me_exp // bit) % 2
        keep = lax.dynamic_index_in_dim(view, mine, axis=2, keepdims=False)
        sent = lax.dynamic_index_in_dim(view, 1 - mine, axis=2, keepdims=False)
        got = lax.ppermute(sent, "exp", [(i, i ^ bit) for i in range(n_exp)])
        reduced = (keep + got).reshape(rows_n, -1, width)
        bit *= 2
    numerator, denominator = reduced[:, :, :-1], reduced[:, :, -1]
    attn_out = (numerator / denominator[:, :, None]).astype(jnp.bfloat16)
    moe_out = routed_experts(tokens, route_ids, route_gates, w_gate, w_up, w_down, attn_out)
    return (attn_out, moe_out)


def solution(mesh):
    return jax.shard_map(
        per_device,
        mesh=mesh,
        in_specs=(
            P("attn", None, None),
            P("attn", None, None),
            P("attn", "exp", None),
            P("attn", None, "exp"),
            P("attn"),
            P(("attn", "exp"), None),
            P(("attn", "exp"), None),
            P(("attn", "exp"), None),
            P("attn", None, "exp"),
            P("attn", None, "exp"),
            P("attn", "exp", None),
        ),
        out_specs=(P("attn", "exp", None), P(("attn", "exp"), None)),
        check_vma=False,
    )
```

```python
import math

import jax
import jax.numpy as jnp
from jax import lax
from jax.sharding import PartitionSpec as P

score_scale = 1.0 / math.sqrt(192.0)
neg_fill = -1e30


def expert_part(row_block, gate_slice, up_slice, down_slice):
    gate_value = jnp.dot(row_block, gate_slice, preferred_element_type=jnp.float32)
    upward = jnp.dot(row_block, up_slice, preferred_element_type=jnp.float32)
    hidden = (jax.nn.silu(gate_value) * upward).astype(jnp.bfloat16)
    return jnp.dot(hidden, down_slice, preferred_element_type=jnp.float32)


def shift_gather(x, axis, n):
    pieces = [x]
    for k in range(1, n):
        pieces.append(lax.ppermute(x, axis, [(i, (i + k) % n) for i in range(n)]))
    return jnp.stack(pieces)


def shift_scatter_sum(q, axis, n):
    total = q[0]
    for k in range(1, n):
        total = total + lax.ppermute(q[k], axis, [(i, (i - k) % n) for i in range(n)])
    return total


def bit_gather(x, axis, bit, n):
    other = lax.ppermute(x, axis, [(i, i ^ bit) for i in range(n)])
    return jnp.stack([x, other])


def bit_reduce(x, axis, bit, n, wire=None):
    sent = x[1] if wire is None else x[1].astype(wire)
    return x[0] + lax.ppermute(sent, axis, [(i, i ^ bit) for i in range(n)]).astype(x.dtype)


def routed_experts(tokens, route_ids, route_gates, w_gate, w_up, w_down, earlier):
    n_exp = lax.axis_size("exp")
    n_attn = lax.axis_size("attn")
    n_local = w_gate.shape[0]
    n_experts = n_attn * n_local
    tok_count, model_width = tokens.shape
    bits = []
    b = n_exp // 2
    while b >= 1:
        bits.append(b)
        b //= 2
    hit = route_ids[:, :, None] == jnp.arange(n_experts, dtype=jnp.int32)[None, None, :]
    wmat = jnp.sum(jnp.where(hit, route_gates[:, :, None], 0.0), axis=1)
    split = max(1, (5 * n_attn) // 8)
    bounds = [0, split, n_attn] if split < n_attn else [0, n_attn]
    n_chunks = len(bounds) - 1
    pieces = [tokens]
    for k in range(1, n_attn):
        pieces.append(lax.ppermute(tokens, "attn", [(s, (s + k) % n_attn) for s in range(n_attn)]))
    blocks = []
    for c in range(n_chunks):
        block = jnp.stack(pieces[bounds[c] : bounds[c + 1]])
        for bit in bits:
            block = bit_gather(block, "exp", bit, n_exp)
        blocks.append(block)
    me = lax.axis_index("attn")
    owners = (me + jnp.arange(n_attn, dtype=jnp.int32)) % n_attn
    result = jnp.zeros((tok_count, model_width), jnp.float32)
    for i in range(n_local):
        chosen = jnp.take(wmat, owners * n_local + i, axis=1)
        for c in range(n_chunks):
            block = blocks[c]
            part = expert_part(block.reshape(-1, model_width), w_gate[i], w_up[i], w_down[i])
            part = part.reshape(block.shape[:-1] + (model_width,))
            for bit in reversed(bits):
                wire = jnp.bfloat16 if bit == bits[0] else None
                part = bit_reduce(part, "exp", bit, n_exp, wire)
            expert_rows = part.astype(jnp.bfloat16)
            for kk in range(bounds[c + 1] - bounds[c]):
                k = bounds[c] + kk
                if k == 0:
                    back = expert_rows[kk]
                else:
                    back = lax.ppermute(
                        expert_rows[kk], "attn", [(s, (s - k) % n_attn) for s in range(n_attn)]
                    )
                result = result + chosen[:, k : k + 1] * back.astype(jnp.float32)
    return result.astype(jnp.bfloat16)

def per_device(
    q_latent,
    q_rope,
    cache_latent,
    cache_rope,
    lengths,
    tokens,
    route_ids,
    route_gates,
    w_gate,
    w_up,
    w_down,
):
    n_exp = lax.axis_size("exp")
    n_attn = lax.axis_size("attn")
    positions = cache_latent.shape[1]
    scores = jnp.einsum("rhl,rpl->rhp", q_latent, cache_latent, preferred_element_type=jnp.float32)
    scores = scores + jnp.einsum(
        "rdh,rdp->rhp", q_rope, cache_rope, preferred_element_type=jnp.float32
    )
    scores = score_scale * scores
    global_pos = lax.axis_index("exp") * positions + jnp.arange(positions, dtype=jnp.int32)
    is_live = global_pos[None, None, :] < lengths[:, None, None]
    masked = jnp.where(is_live, scores, neg_fill)
    block_max = jnp.max(masked, axis=2)
    weights = jnp.where(is_live, jnp.exp(masked - block_max[:, :, None]), 0.0)
    block_sum = jnp.sum(weights, axis=2)
    block_out = jnp.einsum(
        "rhp,rpl->rhl",
        weights.astype(jnp.bfloat16),
        cache_latent,
        preferred_element_type=jnp.float32,
    )
    me_exp = lax.axis_index("exp")
    row_top = block_max
    bit = 1
    while bit < n_exp:
        row_top = jnp.maximum(
            row_top, lax.ppermute(row_top, "exp", [(i, i ^ bit) for i in range(n_exp)])
        )
        bit *= 2
    factor = jnp.exp(block_max - row_top)
    reduced = jnp.concatenate([block_out * factor[:, :, None], (block_sum * factor)[:, :, None]], axis=2)
    rows_n, heads_n, width = reduced.shape
    bit = 1
    while bit < n_exp:
        outer = n_exp // (2 * bit)
        view = reduced.reshape(rows_n, outer, 2, -1, width)
        mine = (me_exp // bit) % 2
        keep = lax.dynamic_index_in_dim(view, mine, axis=2, keepdims=False)
        sent = lax.dynamic_index_in_dim(view, 1 - mine, axis=2, keepdims=False)
        got = lax.ppermute(sent, "exp", [(i, i ^ bit) for i in range(n_exp)])
        reduced = (keep + got).reshape(rows_n, -1, width)
        bit *= 2
    numerator, denominator = reduced[:, :, :-1], reduced[:, :, -1]
    attn_out = (numerator / denominator[:, :, None]).astype(jnp.bfloat16)
    moe_out = routed_experts(tokens, route_ids, route_gates, w_gate, w_up, w_down, attn_out)
    return (attn_out, moe_out)


def solution(mesh):
    return jax.shard_map(
        per_device,
        mesh=mesh,
        in_specs=(
            P("attn", None, None),
            P("attn", None, None),
            P("attn", "exp", None),
            P("attn", None, "exp"),
            P("attn"),
            P(("attn", "exp"), None),
            P(("attn", "exp"), None),
            P(("attn", "exp"), None),
            P("attn", None, "exp"),
            P("attn", None, "exp"),
            P("attn", "exp", None),
        ),
        out_specs=(P("attn", "exp", None), P(("attn", "exp"), None)),
        check_vma=False,
    )
```

```python
import math

import jax
import jax.numpy as jnp
from jax import lax
from jax.sharding import PartitionSpec as P

score_scale = 1.0 / math.sqrt(192.0)
neg_fill = -1e30


def expert_part(row_block, gate_slice, up_slice, down_slice):
    gate_value = jnp.dot(row_block, gate_slice, preferred_element_type=jnp.float32)
    upward = jnp.dot(row_block, up_slice, preferred_element_type=jnp.float32)
    hidden = (jax.nn.silu(gate_value) * upward).astype(jnp.bfloat16)
    return jnp.dot(hidden, down_slice, preferred_element_type=jnp.float32)


def shift_gather(x, axis, n):
    pieces = [x]
    for k in range(1, n):
        pieces.append(lax.ppermute(x, axis, [(i, (i + k) % n) for i in range(n)]))
    return jnp.stack(pieces)


def shift_scatter_sum(q, axis, n):
    total = q[0]
    for k in range(1, n):
        total = total + lax.ppermute(q[k], axis, [(i, (i - k) % n) for i in range(n)])
    return total


def bit_gather(x, axis, bit, n):
    other = lax.ppermute(x, axis, [(i, i ^ bit) for i in range(n)])
    return jnp.stack([x, other])


def bit_reduce(x, axis, bit, n, wire=None):
    sent = x[1] if wire is None else x[1].astype(wire)
    return x[0] + lax.ppermute(sent, axis, [(i, i ^ bit) for i in range(n)]).astype(x.dtype)


def routed_experts(tokens, route_ids, route_gates, w_gate, w_up, w_down, earlier):
    n_exp = lax.axis_size("exp")
    n_attn = lax.axis_size("attn")
    n_local = w_gate.shape[0]
    n_experts = n_attn * n_local
    tok_count, model_width = tokens.shape
    bits = []
    b = n_exp // 2
    while b >= 1:
        bits.append(b)
        b //= 2
    hit = route_ids[:, :, None] == jnp.arange(n_experts, dtype=jnp.int32)[None, None, :]
    wmat = jnp.sum(jnp.where(hit, route_gates[:, :, None], 0.0), axis=1)
    n_chunks = 2 if n_attn % 2 == 0 else 1
    per_chunk = n_attn // n_chunks
    pieces = [tokens]
    for k in range(1, n_attn):
        pieces.append(lax.ppermute(tokens, "attn", [(s, (s + k) % n_attn) for s in range(n_attn)]))
    blocks = []
    for c in range(n_chunks):
        block = jnp.stack(pieces[c * per_chunk : (c + 1) * per_chunk])
        for bit in bits:
            block = bit_gather(block, "exp", bit, n_exp)
        blocks.append(block)
    me = lax.axis_index("attn")
    owners = (me + jnp.arange(n_attn, dtype=jnp.int32)) % n_attn
    result = jnp.zeros((tok_count, model_width), jnp.float32)
    for i in range(n_local):
        chosen = jnp.take(wmat, owners * n_local + i, axis=1)
        both = jnp.concatenate([block.reshape(-1, model_width) for block in blocks], axis=0)
        gate_value = jnp.dot(both, w_gate[i], preferred_element_type=jnp.float32)
        upward = jnp.dot(both, w_up[i], preferred_element_type=jnp.float32)
        hidden = (jax.nn.silu(gate_value) * upward).astype(jnp.bfloat16)
        offset = 0
        for c in range(n_chunks):
            block = blocks[c]
            count = block.size // model_width
            part = jnp.dot(hidden[offset : offset + count], w_down[i], preferred_element_type=jnp.float32)
            offset += count
            part = part.reshape(block.shape[:-1] + (model_width,))
            for bit in reversed(bits):
                wire = jnp.bfloat16 if bit == bits[0] else None
                part = bit_reduce(part, "exp", bit, n_exp, wire)
            expert_rows = part.astype(jnp.bfloat16)
            for kk in range(per_chunk):
                k = c * per_chunk + kk
                if k == 0:
                    back = expert_rows[kk]
                else:
                    back = lax.ppermute(
                        expert_rows[kk], "attn", [(s, (s - k) % n_attn) for s in range(n_attn)]
                    )
                result = result + chosen[:, k : k + 1] * back.astype(jnp.float32)
    return result.astype(jnp.bfloat16)

def per_device(
    q_latent,
    q_rope,
    cache_latent,
    cache_rope,
    lengths,
    tokens,
    route_ids,
    route_gates,
    w_gate,
    w_up,
    w_down,
):
    n_exp = lax.axis_size("exp")
    n_attn = lax.axis_size("attn")
    positions = cache_latent.shape[1]
    scores = jnp.einsum("rhl,rpl->rhp", q_latent, cache_latent, preferred_element_type=jnp.float32)
    scores = scores + jnp.einsum(
        "rdh,rdp->rhp", q_rope, cache_rope, preferred_element_type=jnp.float32
    )
    scores = score_scale * scores
    global_pos = lax.axis_index("exp") * positions + jnp.arange(positions, dtype=jnp.int32)
    is_live = global_pos[None, None, :] < lengths[:, None, None]
    masked = jnp.where(is_live, scores, neg_fill)
    block_max = jnp.max(masked, axis=2)
    weights = jnp.where(is_live, jnp.exp(masked - block_max[:, :, None]), 0.0)
    block_sum = jnp.sum(weights, axis=2)
    block_out = jnp.einsum(
        "rhp,rpl->rhl",
        weights.astype(jnp.bfloat16),
        cache_latent,
        preferred_element_type=jnp.float32,
    )
    me_exp = lax.axis_index("exp")
    row_top = block_max
    bit = 1
    while bit < n_exp:
        row_top = jnp.maximum(
            row_top, lax.ppermute(row_top, "exp", [(i, i ^ bit) for i in range(n_exp)])
        )
        bit *= 2
    factor = jnp.exp(block_max - row_top)
    reduced = jnp.concatenate([block_out * factor[:, :, None], (block_sum * factor)[:, :, None]], axis=2)
    rows_n, heads_n, width = reduced.shape
    bit = 1
    while bit < n_exp:
        outer = n_exp // (2 * bit)
        view = reduced.reshape(rows_n, outer, 2, -1, width)
        mine = (me_exp // bit) % 2
        keep = lax.dynamic_index_in_dim(view, mine, axis=2, keepdims=False)
        sent = lax.dynamic_index_in_dim(view, 1 - mine, axis=2, keepdims=False)
        got = lax.ppermute(sent, "exp", [(i, i ^ bit) for i in range(n_exp)])
        reduced = (keep + got).reshape(rows_n, -1, width)
        bit *= 2
    numerator, denominator = reduced[:, :, :-1], reduced[:, :, -1]
    attn_out = (numerator / denominator[:, :, None]).astype(jnp.bfloat16)
    moe_out = routed_experts(tokens, route_ids, route_gates, w_gate, w_up, w_down, attn_out)
    return (attn_out, moe_out)


def solution(mesh):
    return jax.shard_map(
        per_device,
        mesh=mesh,
        in_specs=(
            P("attn", None, None),
            P("attn", None, None),
            P("attn", "exp", None),
            P("attn", None, "exp"),
            P("attn"),
            P(("attn", "exp"), None),
            P(("attn", "exp"), None),
            P(("attn", "exp"), None),
            P("attn", None, "exp"),
            P("attn", None, "exp"),
            P("attn", "exp", None),
        ),
        out_specs=(P("attn", "exp", None), P(("attn", "exp"), None)),
        check_vma=False,
    )
```

```python
import math

import jax
import jax.numpy as jnp
from jax import lax
from jax.sharding import PartitionSpec as P

score_scale = 1.0 / math.sqrt(192.0)
neg_fill = -1e30


def expert_part(row_block, gate_slice, up_slice, down_slice):
    gate_value = jnp.dot(row_block, gate_slice, preferred_element_type=jnp.float32)
    upward = jnp.dot(row_block, up_slice, preferred_element_type=jnp.float32)
    hidden = (jax.nn.silu(gate_value) * upward).astype(jnp.bfloat16)
    return jnp.dot(hidden, down_slice, preferred_element_type=jnp.float32)


def shift_gather(x, axis, n):
    pieces = [x]
    for k in range(1, n):
        pieces.append(lax.ppermute(x, axis, [(i, (i + k) % n) for i in range(n)]))
    return jnp.stack(pieces)


def shift_scatter_sum(q, axis, n):
    total = q[0]
    for k in range(1, n):
        total = total + lax.ppermute(q[k], axis, [(i, (i - k) % n) for i in range(n)])
    return total


def bit_gather(x, axis, bit, n):
    other = lax.ppermute(x, axis, [(i, i ^ bit) for i in range(n)])
    return jnp.stack([x, other])


def bit_reduce(x, axis, bit, n, wire=None):
    sent = x[1] if wire is None else x[1].astype(wire)
    return x[0] + lax.ppermute(sent, axis, [(i, i ^ bit) for i in range(n)]).astype(x.dtype)


def routed_experts(tokens, route_ids, route_gates, w_gate, w_up, w_down, earlier):
    n_exp = lax.axis_size("exp")
    n_attn = lax.axis_size("attn")
    n_local = w_gate.shape[0]
    n_experts = n_attn * n_local
    tok_count, model_width = tokens.shape
    bits = []
    b = n_exp // 2
    while b >= 1:
        bits.append(b)
        b //= 2
    hit = route_ids[:, :, None] == jnp.arange(n_experts, dtype=jnp.int32)[None, None, :]
    wmat = jnp.sum(jnp.where(hit, route_gates[:, :, None], 0.0), axis=1)
    n_chunks = 2 if n_attn % 2 == 0 else 1
    per_chunk = n_attn // n_chunks
    pieces = [tokens]
    for k in range(1, n_attn):
        pieces.append(lax.ppermute(tokens, "attn", [(s, (s + k) % n_attn) for s in range(n_attn)]))
    blocks = []
    for c in range(n_chunks):
        block = jnp.stack(pieces[c * per_chunk : (c + 1) * per_chunk])
        for bit in bits:
            block = bit_gather(block, "exp", bit, n_exp)
        blocks.append(block)
    me = lax.axis_index("attn")
    owners = (me + jnp.arange(n_attn, dtype=jnp.int32)) % n_attn
    result = jnp.zeros((tok_count, model_width), jnp.float32)
    for i in range(n_local):
        chosen = jnp.take(wmat, owners * n_local + i, axis=1)
        both = jnp.concatenate([block.reshape(-1, model_width) for block in blocks], axis=0)
        gate_value = jnp.dot(both, w_gate[i], preferred_element_type=jnp.float32)
        upward = jnp.dot(both, w_up[i], preferred_element_type=jnp.float32)
        hidden = (jax.nn.silu(gate_value) * upward).astype(jnp.bfloat16)
        down_all = jnp.dot(hidden, w_down[i], preferred_element_type=jnp.float32)
        offset = 0
        for c in range(n_chunks):
            block = blocks[c]
            count = block.size // model_width
            part = down_all[offset : offset + count]
            offset += count
            part = part.reshape(block.shape[:-1] + (model_width,))
            for bit in reversed(bits):
                wire = jnp.bfloat16 if bit == bits[0] else None
                part = bit_reduce(part, "exp", bit, n_exp, wire)
            expert_rows = part.astype(jnp.bfloat16)
            for kk in range(per_chunk):
                k = c * per_chunk + kk
                if k == 0:
                    back = expert_rows[kk]
                else:
                    back = lax.ppermute(
                        expert_rows[kk], "attn", [(s, (s - k) % n_attn) for s in range(n_attn)]
                    )
                result = result + chosen[:, k : k + 1] * back.astype(jnp.float32)
    return result.astype(jnp.bfloat16)

def per_device(
    q_latent,
    q_rope,
    cache_latent,
    cache_rope,
    lengths,
    tokens,
    route_ids,
    route_gates,
    w_gate,
    w_up,
    w_down,
):
    n_exp = lax.axis_size("exp")
    n_attn = lax.axis_size("attn")
    positions = cache_latent.shape[1]
    scores = jnp.einsum("rhl,rpl->rhp", q_latent, cache_latent, preferred_element_type=jnp.float32)
    scores = scores + jnp.einsum(
        "rdh,rdp->rhp", q_rope, cache_rope, preferred_element_type=jnp.float32
    )
    scores = score_scale * scores
    global_pos = lax.axis_index("exp") * positions + jnp.arange(positions, dtype=jnp.int32)
    is_live = global_pos[None, None, :] < lengths[:, None, None]
    masked = jnp.where(is_live, scores, neg_fill)
    block_max = jnp.max(masked, axis=2)
    weights = jnp.where(is_live, jnp.exp(masked - block_max[:, :, None]), 0.0)
    block_sum = jnp.sum(weights, axis=2)
    block_out = jnp.einsum(
        "rhp,rpl->rhl",
        weights.astype(jnp.bfloat16),
        cache_latent,
        preferred_element_type=jnp.float32,
    )
    me_exp = lax.axis_index("exp")
    row_top = block_max
    bit = 1
    while bit < n_exp:
        row_top = jnp.maximum(
            row_top, lax.ppermute(row_top, "exp", [(i, i ^ bit) for i in range(n_exp)])
        )
        bit *= 2
    factor = jnp.exp(block_max - row_top)
    reduced = jnp.concatenate([block_out * factor[:, :, None], (block_sum * factor)[:, :, None]], axis=2)
    rows_n, heads_n, width = reduced.shape
    bit = 1
    while bit < n_exp:
        outer = n_exp // (2 * bit)
        view = reduced.reshape(rows_n, outer, 2, -1, width)
        mine = (me_exp // bit) % 2
        keep = lax.dynamic_index_in_dim(view, mine, axis=2, keepdims=False)
        sent = lax.dynamic_index_in_dim(view, 1 - mine, axis=2, keepdims=False)
        got = lax.ppermute(sent, "exp", [(i, i ^ bit) for i in range(n_exp)])
        reduced = (keep + got).reshape(rows_n, -1, width)
        bit *= 2
    numerator, denominator = reduced[:, :, :-1], reduced[:, :, -1]
    attn_out = (numerator / denominator[:, :, None]).astype(jnp.bfloat16)
    moe_out = routed_experts(tokens, route_ids, route_gates, w_gate, w_up, w_down, attn_out)
    return (attn_out, moe_out)


def solution(mesh):
    return jax.shard_map(
        per_device,
        mesh=mesh,
        in_specs=(
            P("attn", None, None),
            P("attn", None, None),
            P("attn", "exp", None),
            P("attn", None, "exp"),
            P("attn"),
            P(("attn", "exp"), None),
            P(("attn", "exp"), None),
            P(("attn", "exp"), None),
            P("attn", None, "exp"),
            P("attn", None, "exp"),
            P("attn", "exp", None),
        ),
        out_specs=(P("attn", "exp", None), P(("attn", "exp"), None)),
        check_vma=False,
    )
```

```python
import math

import jax
import jax.numpy as jnp
from jax import lax
from jax.sharding import PartitionSpec as P

score_scale = 1.0 / math.sqrt(192.0)
neg_fill = -1e30


def expert_part(row_block, gate_slice, up_slice, down_slice):
    gate_value = jnp.dot(row_block, gate_slice, preferred_element_type=jnp.float32)
    upward = jnp.dot(row_block, up_slice, preferred_element_type=jnp.float32)
    hidden = (jax.nn.silu(gate_value) * upward).astype(jnp.bfloat16)
    return jnp.dot(hidden, down_slice, preferred_element_type=jnp.float32)


def shift_gather(x, axis, n):
    pieces = [x]
    for k in range(1, n):
        pieces.append(lax.ppermute(x, axis, [(i, (i + k) % n) for i in range(n)]))
    return jnp.stack(pieces)


def shift_scatter_sum(q, axis, n):
    total = q[0]
    for k in range(1, n):
        total = total + lax.ppermute(q[k], axis, [(i, (i - k) % n) for i in range(n)])
    return total


def bit_gather(x, axis, bit, n):
    other = lax.ppermute(x, axis, [(i, i ^ bit) for i in range(n)])
    return jnp.stack([x, other])


def bit_reduce(x, axis, bit, n, wire=None):
    sent = x[1] if wire is None else x[1].astype(wire)
    return x[0] + lax.ppermute(sent, axis, [(i, i ^ bit) for i in range(n)]).astype(x.dtype)


def routed_experts(tokens, route_ids, route_gates, w_gate, w_up, w_down, earlier):
    n_exp = lax.axis_size("exp")
    n_attn = lax.axis_size("attn")
    n_local = w_gate.shape[0]
    n_experts = n_attn * n_local
    tok_count, model_width = tokens.shape
    bits = []
    b = n_exp // 2
    while b >= 1:
        bits.append(b)
        b //= 2
    hit = route_ids[:, :, None] == jnp.arange(n_experts, dtype=jnp.int32)[None, None, :]
    wmat = jnp.sum(jnp.where(hit, route_gates[:, :, None], 0.0), axis=1)
    n_chunks = 4 if n_attn % 4 == 0 else 1
    per_chunk = n_attn // n_chunks
    pieces = [tokens]
    for k in range(1, n_attn):
        pieces.append(lax.ppermute(tokens, "attn", [(s, (s + k) % n_attn) for s in range(n_attn)]))
    blocks = []
    for c in range(n_chunks):
        block = jnp.stack(pieces[c * per_chunk : (c + 1) * per_chunk])
        for bit in bits:
            block = bit_gather(block, "exp", bit, n_exp)
        blocks.append(block)
    me = lax.axis_index("attn")
    owners = (me + jnp.arange(n_attn, dtype=jnp.int32)) % n_attn
    result = jnp.zeros((tok_count, model_width), jnp.float32)
    for i in range(n_local):
        chosen = jnp.take(wmat, owners * n_local + i, axis=1)
        both = jnp.concatenate([block.reshape(-1, model_width) for block in blocks], axis=0)
        gate_value = jnp.dot(both, w_gate[i], preferred_element_type=jnp.float32)
        upward = jnp.dot(both, w_up[i], preferred_element_type=jnp.float32)
        hidden = (jax.nn.silu(gate_value) * upward).astype(jnp.bfloat16)
        offset = 0
        for c in range(n_chunks):
            block = blocks[c]
            count = block.size // model_width
            part = jnp.dot(hidden[offset : offset + count], w_down[i], preferred_element_type=jnp.float32)
            offset += count
            part = part.reshape(block.shape[:-1] + (model_width,))
            for bit in reversed(bits):
                wire = jnp.bfloat16 if bit == bits[0] else None
                part = bit_reduce(part, "exp", bit, n_exp, wire)
            expert_rows = part.astype(jnp.bfloat16)
            for kk in range(per_chunk):
                k = c * per_chunk + kk
                if k == 0:
                    back = expert_rows[kk]
                else:
                    back = lax.ppermute(
                        expert_rows[kk], "attn", [(s, (s - k) % n_attn) for s in range(n_attn)]
                    )
                result = result + chosen[:, k : k + 1] * back.astype(jnp.float32)
    return result.astype(jnp.bfloat16)

def per_device(
    q_latent,
    q_rope,
    cache_latent,
    cache_rope,
    lengths,
    tokens,
    route_ids,
    route_gates,
    w_gate,
    w_up,
    w_down,
):
    n_exp = lax.axis_size("exp")
    n_attn = lax.axis_size("attn")
    positions = cache_latent.shape[1]
    scores = jnp.einsum("rhl,rpl->rhp", q_latent, cache_latent, preferred_element_type=jnp.float32)
    scores = scores + jnp.einsum(
        "rdh,rdp->rhp", q_rope, cache_rope, preferred_element_type=jnp.float32
    )
    scores = score_scale * scores
    global_pos = lax.axis_index("exp") * positions + jnp.arange(positions, dtype=jnp.int32)
    is_live = global_pos[None, None, :] < lengths[:, None, None]
    masked = jnp.where(is_live, scores, neg_fill)
    block_max = jnp.max(masked, axis=2)
    weights = jnp.where(is_live, jnp.exp(masked - block_max[:, :, None]), 0.0)
    block_sum = jnp.sum(weights, axis=2)
    block_out = jnp.einsum(
        "rhp,rpl->rhl",
        weights.astype(jnp.bfloat16),
        cache_latent,
        preferred_element_type=jnp.float32,
    )
    me_exp = lax.axis_index("exp")
    row_top = block_max
    bit = 1
    while bit < n_exp:
        row_top = jnp.maximum(
            row_top, lax.ppermute(row_top, "exp", [(i, i ^ bit) for i in range(n_exp)])
        )
        bit *= 2
    factor = jnp.exp(block_max - row_top)
    reduced = jnp.concatenate([block_out * factor[:, :, None], (block_sum * factor)[:, :, None]], axis=2)
    rows_n, heads_n, width = reduced.shape
    bit = 1
    while bit < n_exp:
        outer = n_exp // (2 * bit)
        view = reduced.reshape(rows_n, outer, 2, -1, width)
        mine = (me_exp // bit) % 2
        keep = lax.dynamic_index_in_dim(view, mine, axis=2, keepdims=False)
        sent = lax.dynamic_index_in_dim(view, 1 - mine, axis=2, keepdims=False)
        got = lax.ppermute(sent, "exp", [(i, i ^ bit) for i in range(n_exp)])
        reduced = (keep + got).reshape(rows_n, -1, width)
        bit *= 2
    numerator, denominator = reduced[:, :, :-1], reduced[:, :, -1]
    attn_out = (numerator / denominator[:, :, None]).astype(jnp.bfloat16)
    moe_out = routed_experts(tokens, route_ids, route_gates, w_gate, w_up, w_down, attn_out)
    return (attn_out, moe_out)


def solution(mesh):
    return jax.shard_map(
        per_device,
        mesh=mesh,
        in_specs=(
            P("attn", None, None),
            P("attn", None, None),
            P("attn", "exp", None),
            P("attn", None, "exp"),
            P("attn"),
            P(("attn", "exp"), None),
            P(("attn", "exp"), None),
            P(("attn", "exp"), None),
            P("attn", None, "exp"),
            P("attn", None, "exp"),
            P("attn", "exp", None),
        ),
        out_specs=(P("attn", "exp", None), P(("attn", "exp"), None)),
        check_vma=False,
    )
```

```python
import math

import jax
import jax.numpy as jnp
from jax import lax
from jax.sharding import PartitionSpec as P

score_scale = 1.0 / math.sqrt(192.0)
neg_fill = -1e30


def expert_part(row_block, gate_slice, up_slice, down_slice):
    gate_value = jnp.dot(row_block, gate_slice, preferred_element_type=jnp.float32)
    upward = jnp.dot(row_block, up_slice, preferred_element_type=jnp.float32)
    hidden = (jax.nn.silu(gate_value) * upward).astype(jnp.bfloat16)
    return jnp.dot(hidden, down_slice, preferred_element_type=jnp.float32)


def shift_gather(x, axis, n):
    pieces = [x]
    for k in range(1, n):
        pieces.append(lax.ppermute(x, axis, [(i, (i + k) % n) for i in range(n)]))
    return jnp.stack(pieces)


def shift_scatter_sum(q, axis, n):
    total = q[0]
    for k in range(1, n):
        total = total + lax.ppermute(q[k], axis, [(i, (i - k) % n) for i in range(n)])
    return total


def bit_gather(x, axis, bit, n):
    other = lax.ppermute(x, axis, [(i, i ^ bit) for i in range(n)])
    return jnp.stack([x, other])


def bit_reduce(x, axis, bit, n, wire=None):
    sent = x[1] if wire is None else x[1].astype(wire)
    return x[0] + lax.ppermute(sent, axis, [(i, i ^ bit) for i in range(n)]).astype(x.dtype)


def routed_experts(tokens, route_ids, route_gates, w_gate, w_up, w_down, earlier):
    n_exp = lax.axis_size("exp")
    n_attn = lax.axis_size("attn")
    n_local = w_gate.shape[0]
    n_experts = n_attn * n_local
    tok_count, model_width = tokens.shape
    bits = []
    b = n_exp // 2
    while b >= 1:
        bits.append(b)
        b //= 2
    hit = route_ids[:, :, None] == jnp.arange(n_experts, dtype=jnp.int32)[None, None, :]
    wmat = jnp.sum(jnp.where(hit, route_gates[:, :, None], 0.0), axis=1)
    n_chunks = 2 if n_attn % 2 == 0 else 1
    per_chunk = n_attn // n_chunks
    pieces = [tokens]
    for k in range(1, n_attn):
        pieces.append(lax.ppermute(tokens, "attn", [(s, (s + k) % n_attn) for s in range(n_attn)]))
    blocks = []
    for c in range(n_chunks):
        block = jnp.stack(pieces[c * per_chunk : (c + 1) * per_chunk])
        for bit in bits:
            block = bit_gather(block, "exp", bit, n_exp)
        blocks.append(block)
    me = lax.axis_index("attn")
    owners = (me + jnp.arange(n_attn, dtype=jnp.int32)) % n_attn
    result = jnp.zeros((tok_count, model_width), jnp.float32)
    for i in range(n_local):
        chosen = jnp.take(wmat, owners * n_local + i, axis=1)
        both = jnp.concatenate([block.reshape(-1, model_width) for block in blocks], axis=0)
        gate_value = jnp.dot(both, w_gate[i], preferred_element_type=jnp.float32)
        upward = jnp.dot(both, w_up[i], preferred_element_type=jnp.float32)
        hidden = (jax.nn.silu(gate_value) * upward).astype(jnp.bfloat16)
        offset = 0
        for c in range(n_chunks):
            block = blocks[c]
            count = block.size // model_width
            part = jnp.dot(hidden[offset : offset + count], w_down[i], preferred_element_type=jnp.float32)
            offset += count
            part = part.reshape(block.shape[:-1] + (model_width,))
            for bit in reversed(bits):
                wire = jnp.bfloat16
                part = bit_reduce(part, "exp", bit, n_exp, wire)
            expert_rows = part.astype(jnp.bfloat16)
            for kk in range(per_chunk):
                k = c * per_chunk + kk
                if k == 0:
                    back = expert_rows[kk]
                else:
                    back = lax.ppermute(
                        expert_rows[kk], "attn", [(s, (s - k) % n_attn) for s in range(n_attn)]
                    )
                result = result + chosen[:, k : k + 1] * back.astype(jnp.float32)
    return result.astype(jnp.bfloat16)

def per_device(
    q_latent,
    q_rope,
    cache_latent,
    cache_rope,
    lengths,
    tokens,
    route_ids,
    route_gates,
    w_gate,
    w_up,
    w_down,
):
    n_exp = lax.axis_size("exp")
    n_attn = lax.axis_size("attn")
    positions = cache_latent.shape[1]
    scores = jnp.einsum("rhl,rpl->rhp", q_latent, cache_latent, preferred_element_type=jnp.float32)
    scores = scores + jnp.einsum(
        "rdh,rdp->rhp", q_rope, cache_rope, preferred_element_type=jnp.float32
    )
    scores = score_scale * scores
    global_pos = lax.axis_index("exp") * positions + jnp.arange(positions, dtype=jnp.int32)
    is_live = global_pos[None, None, :] < lengths[:, None, None]
    masked = jnp.where(is_live, scores, neg_fill)
    block_max = jnp.max(masked, axis=2)
    weights = jnp.where(is_live, jnp.exp(masked - block_max[:, :, None]), 0.0)
    block_sum = jnp.sum(weights, axis=2)
    block_out = jnp.einsum(
        "rhp,rpl->rhl",
        weights.astype(jnp.bfloat16),
        cache_latent,
        preferred_element_type=jnp.float32,
    )
    me_exp = lax.axis_index("exp")
    row_top = block_max
    bit = 1
    while bit < n_exp:
        row_top = jnp.maximum(
            row_top, lax.ppermute(row_top, "exp", [(i, i ^ bit) for i in range(n_exp)])
        )
        bit *= 2
    factor = jnp.exp(block_max - row_top)
    reduced = jnp.concatenate([block_out * factor[:, :, None], (block_sum * factor)[:, :, None]], axis=2)
    rows_n, heads_n, width = reduced.shape
    bit = 1
    while bit < n_exp:
        outer = n_exp // (2 * bit)
        view = reduced.reshape(rows_n, outer, 2, -1, width)
        mine = (me_exp // bit) % 2
        keep = lax.dynamic_index_in_dim(view, mine, axis=2, keepdims=False)
        sent = lax.dynamic_index_in_dim(view, 1 - mine, axis=2, keepdims=False)
        got = lax.ppermute(sent, "exp", [(i, i ^ bit) for i in range(n_exp)])
        reduced = (keep + got).reshape(rows_n, -1, width)
        bit *= 2
    numerator, denominator = reduced[:, :, :-1], reduced[:, :, -1]
    attn_out = (numerator / denominator[:, :, None]).astype(jnp.bfloat16)
    moe_out = routed_experts(tokens, route_ids, route_gates, w_gate, w_up, w_down, attn_out)
    return (attn_out, moe_out)


def solution(mesh):
    return jax.shard_map(
        per_device,
        mesh=mesh,
        in_specs=(
            P("attn", None, None),
            P("attn", None, None),
            P("attn", "exp", None),
            P("attn", None, "exp"),
            P("attn"),
            P(("attn", "exp"), None),
            P(("attn", "exp"), None),
            P(("attn", "exp"), None),
            P("attn", None, "exp"),
            P("attn", None, "exp"),
            P("attn", "exp", None),
        ),
        out_specs=(P("attn", "exp", None), P(("attn", "exp"), None)),
        check_vma=False,
    )
```

```python
import math

import jax
import jax.numpy as jnp
from jax import lax
from jax.sharding import PartitionSpec as P

score_scale = 1.0 / math.sqrt(192.0)
neg_fill = -1e30


def expert_part(row_block, gate_slice, up_slice, down_slice):
    gate_value = jnp.dot(row_block, gate_slice, preferred_element_type=jnp.float32)
    upward = jnp.dot(row_block, up_slice, preferred_element_type=jnp.float32)
    hidden = (jax.nn.silu(gate_value) * upward).astype(jnp.bfloat16)
    return jnp.dot(hidden, down_slice, preferred_element_type=jnp.float32)


def shift_gather(x, axis, n):
    pieces = [x]
    for k in range(1, n):
        pieces.append(lax.ppermute(x, axis, [(i, (i + k) % n) for i in range(n)]))
    return jnp.stack(pieces)


def shift_scatter_sum(q, axis, n):
    total = q[0]
    for k in range(1, n):
        total = total + lax.ppermute(q[k], axis, [(i, (i - k) % n) for i in range(n)])
    return total


def bit_gather(x, axis, bit, n):
    other = lax.ppermute(x, axis, [(i, i ^ bit) for i in range(n)])
    return jnp.stack([x, other])


def bit_reduce(x, axis, bit, n, wire=None):
    sent = x[1] if wire is None else x[1].astype(wire)
    return x[0] + lax.ppermute(sent, axis, [(i, i ^ bit) for i in range(n)]).astype(x.dtype)


def routed_experts(tokens, route_ids, route_gates, w_gate, w_up, w_down, earlier):
    n_exp = lax.axis_size("exp")
    n_attn = lax.axis_size("attn")
    n_local = w_gate.shape[0]
    n_experts = n_attn * n_local
    tok_count, model_width = tokens.shape
    bits = []
    b = n_exp // 2
    while b >= 1:
        bits.append(b)
        b //= 2
    hit = route_ids[:, :, None] == jnp.arange(n_experts, dtype=jnp.int32)[None, None, :]
    wmat = jnp.sum(jnp.where(hit, route_gates[:, :, None], 0.0), axis=1)
    n_chunks = 2 if n_attn % 2 == 0 else 1
    per_chunk = n_attn // n_chunks
    pieces = [tokens]
    for k in range(1, n_attn):
        pieces.append(lax.ppermute(tokens, "attn", [(s, (s + k) % n_attn) for s in range(n_attn)]))
    blocks = []
    for c in range(n_chunks):
        block = jnp.stack(pieces[c * per_chunk : (c + 1) * per_chunk])
        for bit in bits:
            block = bit_gather(block, "exp", bit, n_exp)
        blocks.append(block)
    me = lax.axis_index("attn")
    owners = (me + jnp.arange(n_attn, dtype=jnp.int32)) % n_attn
    result = jnp.zeros((tok_count, model_width), jnp.float32)
    for i in range(n_local):
        chosen = jnp.take(wmat, owners * n_local + i, axis=1)
        both = jnp.concatenate([block.reshape(-1, model_width) for block in blocks], axis=0)
        gate_value = jnp.dot(both, w_gate[i], preferred_element_type=jnp.float32)
        upward = jnp.dot(both, w_up[i], preferred_element_type=jnp.float32)
        hidden = (jax.nn.silu(gate_value) * upward).astype(jnp.bfloat16)
        count = blocks[0].size // model_width
        previous = None
        for c in reversed(range(n_chunks)):
            block = blocks[c]
            rows_in = hidden[c * count : (c + 1) * count]
            if previous is not None:
                rows_in, _ = lax.optimization_barrier((rows_in, previous))
            part = jnp.dot(rows_in, w_down[i], preferred_element_type=jnp.float32)
            previous = part
            part = part.reshape(block.shape[:-1] + (model_width,))
            for bit in reversed(bits):
                wire = jnp.bfloat16 if bit == bits[0] else None
                part = bit_reduce(part, "exp", bit, n_exp, wire)
            expert_rows = part.astype(jnp.bfloat16)
            for kk in range(per_chunk):
                k = c * per_chunk + kk
                if k == 0:
                    back = expert_rows[kk]
                else:
                    back = lax.ppermute(
                        expert_rows[kk], "attn", [(s, (s - k) % n_attn) for s in range(n_attn)]
                    )
                result = result + chosen[:, k : k + 1] * back.astype(jnp.float32)
    return result.astype(jnp.bfloat16)

def per_device(
    q_latent,
    q_rope,
    cache_latent,
    cache_rope,
    lengths,
    tokens,
    route_ids,
    route_gates,
    w_gate,
    w_up,
    w_down,
):
    n_exp = lax.axis_size("exp")
    n_attn = lax.axis_size("attn")
    positions = cache_latent.shape[1]
    scores = jnp.einsum("rhl,rpl->rhp", q_latent, cache_latent, preferred_element_type=jnp.float32)
    scores = scores + jnp.einsum(
        "rdh,rdp->rhp", q_rope, cache_rope, preferred_element_type=jnp.float32
    )
    scores = score_scale * scores
    global_pos = lax.axis_index("exp") * positions + jnp.arange(positions, dtype=jnp.int32)
    is_live = global_pos[None, None, :] < lengths[:, None, None]
    masked = jnp.where(is_live, scores, neg_fill)
    block_max = jnp.max(masked, axis=2)
    weights = jnp.where(is_live, jnp.exp(masked - block_max[:, :, None]), 0.0)
    block_sum = jnp.sum(weights, axis=2)
    block_out = jnp.einsum(
        "rhp,rpl->rhl",
        weights.astype(jnp.bfloat16),
        cache_latent,
        preferred_element_type=jnp.float32,
    )
    me_exp = lax.axis_index("exp")
    row_top = block_max
    bit = 1
    while bit < n_exp:
        row_top = jnp.maximum(
            row_top, lax.ppermute(row_top, "exp", [(i, i ^ bit) for i in range(n_exp)])
        )
        bit *= 2
    factor = jnp.exp(block_max - row_top)
    reduced = jnp.concatenate([block_out * factor[:, :, None], (block_sum * factor)[:, :, None]], axis=2)
    rows_n, heads_n, width = reduced.shape
    bit = 1
    while bit < n_exp:
        outer = n_exp // (2 * bit)
        view = reduced.reshape(rows_n, outer, 2, -1, width)
        mine = (me_exp // bit) % 2
        keep = lax.dynamic_index_in_dim(view, mine, axis=2, keepdims=False)
        sent = lax.dynamic_index_in_dim(view, 1 - mine, axis=2, keepdims=False)
        got = lax.ppermute(sent, "exp", [(i, i ^ bit) for i in range(n_exp)])
        reduced = (keep + got).reshape(rows_n, -1, width)
        bit *= 2
    numerator, denominator = reduced[:, :, :-1], reduced[:, :, -1]
    attn_out = (numerator / denominator[:, :, None]).astype(jnp.bfloat16)
    moe_out = routed_experts(tokens, route_ids, route_gates, w_gate, w_up, w_down, attn_out)
    return (attn_out, moe_out)


def solution(mesh):
    return jax.shard_map(
        per_device,
        mesh=mesh,
        in_specs=(
            P("attn", None, None),
            P("attn", None, None),
            P("attn", "exp", None),
            P("attn", None, "exp"),
            P("attn"),
            P(("attn", "exp"), None),
            P(("attn", "exp"), None),
            P(("attn", "exp"), None),
            P("attn", None, "exp"),
            P("attn", None, "exp"),
            P("attn", "exp", None),
        ),
        out_specs=(P("attn", "exp", None), P(("attn", "exp"), None)),
        check_vma=False,
    )
```

```python
import math

import jax
import jax.numpy as jnp
from jax import lax
from jax.sharding import PartitionSpec as P

score_scale = 1.0 / math.sqrt(192.0)
neg_fill = -1e30


def expert_part(row_block, gate_slice, up_slice, down_slice):
    gate_value = jnp.dot(row_block, gate_slice, preferred_element_type=jnp.float32)
    upward = jnp.dot(row_block, up_slice, preferred_element_type=jnp.float32)
    hidden = (jax.nn.silu(gate_value) * upward).astype(jnp.bfloat16)
    return jnp.dot(hidden, down_slice, preferred_element_type=jnp.float32)


def shift_gather(x, axis, n):
    pieces = [x]
    for k in range(1, n):
        pieces.append(lax.ppermute(x, axis, [(i, (i + k) % n) for i in range(n)]))
    return jnp.stack(pieces)


def shift_scatter_sum(q, axis, n):
    total = q[0]
    for k in range(1, n):
        total = total + lax.ppermute(q[k], axis, [(i, (i - k) % n) for i in range(n)])
    return total


def bit_gather(x, axis, bit, n):
    other = lax.ppermute(x, axis, [(i, i ^ bit) for i in range(n)])
    return jnp.stack([x, other])


def bit_reduce(x, axis, bit, n, wire=None):
    sent = x[1] if wire is None else x[1].astype(wire)
    return x[0] + lax.ppermute(sent, axis, [(i, i ^ bit) for i in range(n)]).astype(x.dtype)


def routed_experts(tokens, route_ids, route_gates, w_gate, w_up, w_down, earlier):
    n_exp = lax.axis_size("exp")
    n_attn = lax.axis_size("attn")
    n_local = w_gate.shape[0]
    n_experts = n_attn * n_local
    tok_count, model_width = tokens.shape
    bits = []
    b = n_exp // 2
    while b >= 1:
        bits.append(b)
        b //= 2
    hit = route_ids[:, :, None] == jnp.arange(n_experts, dtype=jnp.int32)[None, None, :]
    wmat = jnp.sum(jnp.where(hit, route_gates[:, :, None], 0.0), axis=1)
    split = max(1, (3 * n_attn) // 8)
    bounds = [0, split, n_attn] if split < n_attn else [0, n_attn]
    n_chunks = len(bounds) - 1
    pieces = [tokens]
    for k in range(1, n_attn):
        pieces.append(lax.ppermute(tokens, "attn", [(s, (s + k) % n_attn) for s in range(n_attn)]))
    blocks = []
    for c in range(n_chunks):
        block = jnp.stack(pieces[bounds[c] : bounds[c + 1]])
        for bit in bits:
            block = bit_gather(block, "exp", bit, n_exp)
        blocks.append(block)
    me = lax.axis_index("attn")
    owners = (me + jnp.arange(n_attn, dtype=jnp.int32)) % n_attn
    result = jnp.zeros((tok_count, model_width), jnp.float32)
    for i in range(n_local):
        chosen = jnp.take(wmat, owners * n_local + i, axis=1)
        both = jnp.concatenate([block.reshape(-1, model_width) for block in blocks], axis=0)
        gate_value = jnp.dot(both, w_gate[i], preferred_element_type=jnp.float32)
        upward = jnp.dot(both, w_up[i], preferred_element_type=jnp.float32)
        hidden = (jax.nn.silu(gate_value) * upward).astype(jnp.bfloat16)
        offset = 0
        for c in range(n_chunks):
            block = blocks[c]
            count = block.size // model_width
            part = jnp.dot(hidden[offset : offset + count], w_down[i], preferred_element_type=jnp.float32)
            offset += count
            part = part.reshape(block.shape[:-1] + (model_width,))
            for bit in reversed(bits):
                wire = jnp.bfloat16 if bit == bits[0] else None
                part = bit_reduce(part, "exp", bit, n_exp, wire)
            expert_rows = part.astype(jnp.bfloat16)
            for kk in range(bounds[c + 1] - bounds[c]):
                k = bounds[c] + kk
                if k == 0:
                    back = expert_rows[kk]
                else:
                    back = lax.ppermute(
                        expert_rows[kk], "attn", [(s, (s - k) % n_attn) for s in range(n_attn)]
                    )
                result = result + chosen[:, k : k + 1] * back.astype(jnp.float32)
    return result.astype(jnp.bfloat16)

def per_device(
    q_latent,
    q_rope,
    cache_latent,
    cache_rope,
    lengths,
    tokens,
    route_ids,
    route_gates,
    w_gate,
    w_up,
    w_down,
):
    n_exp = lax.axis_size("exp")
    n_attn = lax.axis_size("attn")
    positions = cache_latent.shape[1]
    scores = jnp.einsum("rhl,rpl->rhp", q_latent, cache_latent, preferred_element_type=jnp.float32)
    scores = scores + jnp.einsum(
        "rdh,rdp->rhp", q_rope, cache_rope, preferred_element_type=jnp.float32
    )
    scores = score_scale * scores
    global_pos = lax.axis_index("exp") * positions + jnp.arange(positions, dtype=jnp.int32)
    is_live = global_pos[None, None, :] < lengths[:, None, None]
    masked = jnp.where(is_live, scores, neg_fill)
    block_max = jnp.max(masked, axis=2)
    weights = jnp.where(is_live, jnp.exp(masked - block_max[:, :, None]), 0.0)
    block_sum = jnp.sum(weights, axis=2)
    block_out = jnp.einsum(
        "rhp,rpl->rhl",
        weights.astype(jnp.bfloat16),
        cache_latent,
        preferred_element_type=jnp.float32,
    )
    me_exp = lax.axis_index("exp")
    row_top = block_max
    bit = 1
    while bit < n_exp:
        row_top = jnp.maximum(
            row_top, lax.ppermute(row_top, "exp", [(i, i ^ bit) for i in range(n_exp)])
        )
        bit *= 2
    factor = jnp.exp(block_max - row_top)
    reduced = jnp.concatenate([block_out * factor[:, :, None], (block_sum * factor)[:, :, None]], axis=2)
    rows_n, heads_n, width = reduced.shape
    bit = 1
    while bit < n_exp:
        outer = n_exp // (2 * bit)
        view = reduced.reshape(rows_n, outer, 2, -1, width)
        mine = (me_exp // bit) % 2
        keep = lax.dynamic_index_in_dim(view, mine, axis=2, keepdims=False)
        sent = lax.dynamic_index_in_dim(view, 1 - mine, axis=2, keepdims=False)
        got = lax.ppermute(sent, "exp", [(i, i ^ bit) for i in range(n_exp)])
        reduced = (keep + got).reshape(rows_n, -1, width)
        bit *= 2
    numerator, denominator = reduced[:, :, :-1], reduced[:, :, -1]
    attn_out = (numerator / denominator[:, :, None]).astype(jnp.bfloat16)
    moe_out = routed_experts(tokens, route_ids, route_gates, w_gate, w_up, w_down, attn_out)
    return (attn_out, moe_out)


def solution(mesh):
    return jax.shard_map(
        per_device,
        mesh=mesh,
        in_specs=(
            P("attn", None, None),
            P("attn", None, None),
            P("attn", "exp", None),
            P("attn", None, "exp"),
            P("attn"),
            P(("attn", "exp"), None),
            P(("attn", "exp"), None),
            P(("attn", "exp"), None),
            P("attn", None, "exp"),
            P("attn", None, "exp"),
            P("attn", "exp", None),
        ),
        out_specs=(P("attn", "exp", None), P(("attn", "exp"), None)),
        check_vma=False,
    )
```

```python
import math

import jax
import jax.numpy as jnp
from jax import lax
from jax.sharding import PartitionSpec as P

score_scale = 1.0 / math.sqrt(192.0)
neg_fill = -1e30


def expert_part(row_block, gate_slice, up_slice, down_slice):
    gate_value = jnp.dot(row_block, gate_slice, preferred_element_type=jnp.float32)
    upward = jnp.dot(row_block, up_slice, preferred_element_type=jnp.float32)
    hidden = (jax.nn.silu(gate_value) * upward).astype(jnp.bfloat16)
    return jnp.dot(hidden, down_slice, preferred_element_type=jnp.float32)


def shift_gather(x, axis, n):
    pieces = [x]
    for k in range(1, n):
        pieces.append(lax.ppermute(x, axis, [(i, (i + k) % n) for i in range(n)]))
    return jnp.stack(pieces)


def shift_scatter_sum(q, axis, n):
    total = q[0]
    for k in range(1, n):
        total = total + lax.ppermute(q[k], axis, [(i, (i - k) % n) for i in range(n)])
    return total


def bit_gather(x, axis, bit, n):
    other = lax.ppermute(x, axis, [(i, i ^ bit) for i in range(n)])
    return jnp.stack([x, other])


def bit_reduce(x, axis, bit, n, wire=None):
    sent = x[1] if wire is None else x[1].astype(wire)
    return x[0] + lax.ppermute(sent, axis, [(i, i ^ bit) for i in range(n)]).astype(x.dtype)


def routed_experts(tokens, route_ids, route_gates, w_gate, w_up, w_down, earlier):
    n_exp = lax.axis_size("exp")
    n_attn = lax.axis_size("attn")
    n_local = w_gate.shape[0]
    n_experts = n_attn * n_local
    tok_count, model_width = tokens.shape
    bits = []
    b = n_exp // 2
    while b >= 1:
        bits.append(b)
        b //= 2
    hit = route_ids[:, :, None] == jnp.arange(n_experts, dtype=jnp.int32)[None, None, :]
    wmat = jnp.sum(jnp.where(hit, route_gates[:, :, None], 0.0), axis=1)
    n_chunks = 2 if n_attn % 2 == 0 else 1
    per_chunk = n_attn // n_chunks
    pieces = [tokens]
    for k in range(1, n_attn):
        pieces.append(lax.ppermute(tokens, "attn", [(s, (s + k) % n_attn) for s in range(n_attn)]))
    blocks = []
    for c in range(n_chunks):
        block = jnp.stack(pieces[c * per_chunk : (c + 1) * per_chunk])
        for bit in bits:
            block = bit_gather(block, "exp", bit, n_exp)
        blocks.append(block)
    me = lax.axis_index("attn")
    owners = (me + jnp.arange(n_attn, dtype=jnp.int32)) % n_attn
    result = jnp.zeros((tok_count, model_width), jnp.float32)
    for i in range(n_local):
        chosen = jnp.take(wmat, owners * n_local + i, axis=1)
        both = jnp.concatenate([block.reshape(-1, model_width) for block in blocks], axis=0)
        gate_value = jnp.dot(both, w_gate[i], preferred_element_type=jnp.float32)
        upward = jnp.dot(both, w_up[i], preferred_element_type=jnp.float32)
        hidden = (jax.nn.silu(gate_value) * upward).astype(jnp.bfloat16)
        offset = 0
        sub = 2 if per_chunk % 2 == 0 else 1
        width_k = per_chunk // sub
        for piece in range(n_chunks * sub):
            c, s = divmod(piece, sub)
            block = blocks[c]
            count = block.size // model_width
            lead = block.shape[:-1]
            chunk_hidden = hidden[c * count : (c + 1) * count].reshape(lead + (-1,))
            chunk_hidden = lax.slice_in_dim(chunk_hidden, s * width_k, (s + 1) * width_k, axis=len(bits))
            sub_lead = chunk_hidden.shape[:-1]
            part = jnp.dot(chunk_hidden.reshape(-1, chunk_hidden.shape[-1]), w_down[i], preferred_element_type=jnp.float32)
            part = part.reshape(sub_lead + (model_width,))
            for bit in reversed(bits):
                wire = jnp.bfloat16 if bit == bits[0] else None
                part = bit_reduce(part, "exp", bit, n_exp, wire)
            expert_rows = part.astype(jnp.bfloat16)
            for kk in range(width_k):
                k = c * per_chunk + s * width_k + kk
                if k == 0:
                    back = expert_rows[kk]
                else:
                    back = lax.ppermute(
                        expert_rows[kk], "attn", [(s, (s - k) % n_attn) for s in range(n_attn)]
                    )
                result = result + chosen[:, k : k + 1] * back.astype(jnp.float32)
    return result.astype(jnp.bfloat16)

def per_device(
    q_latent,
    q_rope,
    cache_latent,
    cache_rope,
    lengths,
    tokens,
    route_ids,
    route_gates,
    w_gate,
    w_up,
    w_down,
):
    n_exp = lax.axis_size("exp")
    n_attn = lax.axis_size("attn")
    positions = cache_latent.shape[1]
    scores = jnp.einsum("rhl,rpl->rhp", q_latent, cache_latent, preferred_element_type=jnp.float32)
    scores = scores + jnp.einsum(
        "rdh,rdp->rhp", q_rope, cache_rope, preferred_element_type=jnp.float32
    )
    scores = score_scale * scores
    global_pos = lax.axis_index("exp") * positions + jnp.arange(positions, dtype=jnp.int32)
    is_live = global_pos[None, None, :] < lengths[:, None, None]
    masked = jnp.where(is_live, scores, neg_fill)
    block_max = jnp.max(masked, axis=2)
    weights = jnp.where(is_live, jnp.exp(masked - block_max[:, :, None]), 0.0)
    block_sum = jnp.sum(weights, axis=2)
    block_out = jnp.einsum(
        "rhp,rpl->rhl",
        weights.astype(jnp.bfloat16),
        cache_latent,
        preferred_element_type=jnp.float32,
    )
    me_exp = lax.axis_index("exp")
    row_top = block_max
    bit = 1
    while bit < n_exp:
        row_top = jnp.maximum(
            row_top, lax.ppermute(row_top, "exp", [(i, i ^ bit) for i in range(n_exp)])
        )
        bit *= 2
    factor = jnp.exp(block_max - row_top)
    reduced = jnp.concatenate([block_out * factor[:, :, None], (block_sum * factor)[:, :, None]], axis=2)
    rows_n, heads_n, width = reduced.shape
    bit = 1
    while bit < n_exp:
        outer = n_exp // (2 * bit)
        view = reduced.reshape(rows_n, outer, 2, -1, width)
        mine = (me_exp // bit) % 2
        keep = lax.dynamic_index_in_dim(view, mine, axis=2, keepdims=False)
        sent = lax.dynamic_index_in_dim(view, 1 - mine, axis=2, keepdims=False)
        got = lax.ppermute(sent, "exp", [(i, i ^ bit) for i in range(n_exp)])
        reduced = (keep + got).reshape(rows_n, -1, width)
        bit *= 2
    numerator, denominator = reduced[:, :, :-1], reduced[:, :, -1]
    attn_out = (numerator / denominator[:, :, None]).astype(jnp.bfloat16)
    moe_out = routed_experts(tokens, route_ids, route_gates, w_gate, w_up, w_down, attn_out)
    return (attn_out, moe_out)


def solution(mesh):
    return jax.shard_map(
        per_device,
        mesh=mesh,
        in_specs=(
            P("attn", None, None),
            P("attn", None, None),
            P("attn", "exp", None),
            P("attn", None, "exp"),
            P("attn"),
            P(("attn", "exp"), None),
            P(("attn", "exp"), None),
            P(("attn", "exp"), None),
            P("attn", None, "exp"),
            P("attn", None, "exp"),
            P("attn", "exp", None),
        ),
        out_specs=(P("attn", "exp", None), P(("attn", "exp"), None)),
        check_vma=False,
    )
```

```python
import math

import jax
import jax.numpy as jnp
from jax import lax
from jax.sharding import PartitionSpec as P

score_scale = 1.0 / math.sqrt(192.0)
neg_fill = -1e30


def expert_part(row_block, gate_slice, up_slice, down_slice):
    gate_value = jnp.dot(row_block, gate_slice, preferred_element_type=jnp.float32)
    upward = jnp.dot(row_block, up_slice, preferred_element_type=jnp.float32)
    hidden = (jax.nn.silu(gate_value) * upward).astype(jnp.bfloat16)
    return jnp.dot(hidden, down_slice, preferred_element_type=jnp.float32)


def shift_gather(x, axis, n):
    pieces = [x]
    for k in range(1, n):
        pieces.append(lax.ppermute(x, axis, [(i, (i + k) % n) for i in range(n)]))
    return jnp.stack(pieces)


def shift_scatter_sum(q, axis, n):
    total = q[0]
    for k in range(1, n):
        total = total + lax.ppermute(q[k], axis, [(i, (i - k) % n) for i in range(n)])
    return total


def bit_gather(x, axis, bit, n):
    other = lax.ppermute(x, axis, [(i, i ^ bit) for i in range(n)])
    return jnp.stack([x, other])


def bit_reduce(x, axis, bit, n, wire=None):
    sent = x[1] if wire is None else x[1].astype(wire)
    return x[0] + lax.ppermute(sent, axis, [(i, i ^ bit) for i in range(n)]).astype(x.dtype)


def routed_experts(tokens, route_ids, route_gates, w_gate, w_up, w_down, earlier):
    n_exp = lax.axis_size("exp")
    n_attn = lax.axis_size("attn")
    n_local = w_gate.shape[0]
    n_experts = n_attn * n_local
    tok_count, model_width = tokens.shape
    bits = []
    b = n_exp // 2
    while b >= 1:
        bits.append(b)
        b //= 2
    hit = route_ids[:, :, None] == jnp.arange(n_experts, dtype=jnp.int32)[None, None, :]
    wmat = jnp.sum(jnp.where(hit, route_gates[:, :, None], 0.0), axis=1)
    n_chunks = 2 if n_attn % 2 == 0 else 1
    per_chunk = n_attn // n_chunks
    order = sorted(range(n_attn), key=lambda k: (min(k, n_attn - k), -k))
    pieces = [tokens]
    for k in range(1, n_attn):
        pieces.append(lax.ppermute(tokens, "attn", [(s, (s + k) % n_attn) for s in range(n_attn)]))
    blocks = []
    for c in range(n_chunks):
        block = jnp.stack([pieces[k] for k in order[c * per_chunk : (c + 1) * per_chunk]])
        for bit in bits:
            block = bit_gather(block, "exp", bit, n_exp)
        blocks.append(block)
    me = lax.axis_index("attn")
    owners = (me + jnp.arange(n_attn, dtype=jnp.int32)) % n_attn
    result = jnp.zeros((tok_count, model_width), jnp.float32)
    for i in range(n_local):
        chosen = jnp.take(wmat, owners * n_local + i, axis=1)
        both = jnp.concatenate([block.reshape(-1, model_width) for block in blocks], axis=0)
        gate_value = jnp.dot(both, w_gate[i], preferred_element_type=jnp.float32)
        upward = jnp.dot(both, w_up[i], preferred_element_type=jnp.float32)
        hidden = (jax.nn.silu(gate_value) * upward).astype(jnp.bfloat16)
        offset = 0
        for c in range(n_chunks):
            block = blocks[c]
            count = block.size // model_width
            part = jnp.dot(hidden[offset : offset + count], w_down[i], preferred_element_type=jnp.float32)
            offset += count
            part = part.reshape(block.shape[:-1] + (model_width,))
            for bit in reversed(bits):
                wire = jnp.bfloat16 if bit == bits[0] else None
                part = bit_reduce(part, "exp", bit, n_exp, wire)
            expert_rows = part.astype(jnp.bfloat16)
            for kk in range(per_chunk):
                k = order[c * per_chunk + kk]
                if k == 0:
                    back = expert_rows[kk]
                else:
                    back = lax.ppermute(
                        expert_rows[kk], "attn", [(s, (s - k) % n_attn) for s in range(n_attn)]
                    )
                result = result + chosen[:, k : k + 1] * back.astype(jnp.float32)
    return result.astype(jnp.bfloat16)

def per_device(
    q_latent,
    q_rope,
    cache_latent,
    cache_rope,
    lengths,
    tokens,
    route_ids,
    route_gates,
    w_gate,
    w_up,
    w_down,
):
    n_exp = lax.axis_size("exp")
    n_attn = lax.axis_size("attn")
    positions = cache_latent.shape[1]
    scores = jnp.einsum("rhl,rpl->rhp", q_latent, cache_latent, preferred_element_type=jnp.float32)
    scores = scores + jnp.einsum(
        "rdh,rdp->rhp", q_rope, cache_rope, preferred_element_type=jnp.float32
    )
    scores = score_scale * scores
    global_pos = lax.axis_index("exp") * positions + jnp.arange(positions, dtype=jnp.int32)
    is_live = global_pos[None, None, :] < lengths[:, None, None]
    masked = jnp.where(is_live, scores, neg_fill)
    block_max = jnp.max(masked, axis=2)
    weights = jnp.where(is_live, jnp.exp(masked - block_max[:, :, None]), 0.0)
    block_sum = jnp.sum(weights, axis=2)
    block_out = jnp.einsum(
        "rhp,rpl->rhl",
        weights.astype(jnp.bfloat16),
        cache_latent,
        preferred_element_type=jnp.float32,
    )
    me_exp = lax.axis_index("exp")
    row_top = block_max
    bit = 1
    while bit < n_exp:
        row_top = jnp.maximum(
            row_top, lax.ppermute(row_top, "exp", [(i, i ^ bit) for i in range(n_exp)])
        )
        bit *= 2
    factor = jnp.exp(block_max - row_top)
    reduced = jnp.concatenate([block_out * factor[:, :, None], (block_sum * factor)[:, :, None]], axis=2)
    rows_n, heads_n, width = reduced.shape
    bit = 1
    while bit < n_exp:
        outer = n_exp // (2 * bit)
        view = reduced.reshape(rows_n, outer, 2, -1, width)
        mine = (me_exp // bit) % 2
        keep = lax.dynamic_index_in_dim(view, mine, axis=2, keepdims=False)
        sent = lax.dynamic_index_in_dim(view, 1 - mine, axis=2, keepdims=False)
        got = lax.ppermute(sent, "exp", [(i, i ^ bit) for i in range(n_exp)])
        reduced = (keep + got).reshape(rows_n, -1, width)
        bit *= 2
    numerator, denominator = reduced[:, :, :-1], reduced[:, :, -1]
    attn_out = (numerator / denominator[:, :, None]).astype(jnp.bfloat16)
    moe_out = routed_experts(tokens, route_ids, route_gates, w_gate, w_up, w_down, attn_out)
    return (attn_out, moe_out)


def solution(mesh):
    return jax.shard_map(
        per_device,
        mesh=mesh,
        in_specs=(
            P("attn", None, None),
            P("attn", None, None),
            P("attn", "exp", None),
            P("attn", None, "exp"),
            P("attn"),
            P(("attn", "exp"), None),
            P(("attn", "exp"), None),
            P(("attn", "exp"), None),
            P("attn", None, "exp"),
            P("attn", None, "exp"),
            P("attn", "exp", None),
        ),
        out_specs=(P("attn", "exp", None), P(("attn", "exp"), None)),
        check_vma=False,
    )
```
